256 devices in a mesh: ctx: 64 (over x, y_hi, z), pipe: 4 (over y_lo, core).
Axes of the slice: x: 4, y: 4 (y_hi: 2, y_lo: 2; y = y_hi * 2 + y_lo), z: 8, core: 2. Of those that a mesh axis runs over, the one named last changes fastest.
Arguments:
- inputs: bfloat16 [4, 8192, 4096], P('pipe', 'ctx'), may hold values from -16 to 16
- q_raw: bfloat16 [4, 8192, 2048], P('pipe', 'ctx'), may hold values from -6 to 6
- grad_out: bfloat16 [4, 8192, 2048], P('pipe', 'ctx'), may hold values from -6 to 6
- segments: int32 [4, 8192], P('pipe'), may hold values from 0 to 4, never falling along the last dimension, each value on 1 to 3072 neighbouring positions
- w_key: bfloat16 [4, 4096, 512], P('pipe', 'ctx'), may hold values from -0.09375 to 0.09375
- w_value: bfloat16 [4, 4096, 512], P('pipe', 'ctx'), may hold values from -0.09375 to 0.09375
- q_gain: float32 [4, 128], P('pipe'), may hold values from 0.1 to 1.9
- k_gain: float32 [4, 128], P('pipe'), may hold values from 0.1 to 1.9
Outputs:
- query_grad: bfloat16 [4, 8192, 2048], P('pipe', 'ctx')
- key_weight_grad: float32 [4, 4096, 512], P('pipe', 'ctx')
- value_weight_grad: float32 [4, 4096, 512], P('pipe', 'ctx')
- section_grad: bfloat16 [4, 8192, 4096], P('pipe', 'ctx')
The draws below stay inside these ranges and needn't reach their ends.
Inputs may be any that keep to these rules, and one draw needn't show every extreme that they name: `segments`: along each section's sequence the document numbers never fall; every document has 1 to 3072 tokens and one has exactly 3072.
All inputs are finite; a program needn't handle non-finite values.
Results may differ from the reference program's by a relative error of at most 0.019.
Values may be sent and summed in bfloat16 or wider, within the bound.
No kernel may reach another device: no remote copies, remote signals or barrier semaphores. Data moves between devices by JAX's collectives and lax.ppermute only.
A program may use at most 128 MiB of HBM per device.

```python
import math
import jax
import jax.numpy as jnp
import numpy as np
from jax import lax

D = 4096
HEAD = 128
QHEADS = 16
WINDOW = 768
TOK_DEV = 128
SECTIONS = 4
TOKENS = 8192
KVW = 512
DOCS = 5
DOC_MOST = 3072


def spiked(entries, stream_key, source, target, parts, factor):
    owner, partner = [(jnp.arange(entries.shape[axis_at]) // (entries.shape[axis_at] // parts)).reshape([-1 if axis == axis_at else 1 for axis in range(entries.ndim)]) for axis_at in (source, target)]
    chosen = jax.random.permutation(stream_key, parts)[partner]
    strong = (owner == chosen) | (owner == (partner + parts // 2) % parts)
    return jnp.where(strong, factor * entries, entries)


def levels(key, dims, shards, smallest, high):
    gain, own = 1.0, jax.random.fold_in(key, 6)
    for position, shards_of in shards:
        steps = jnp.exp(jax.random.uniform(jax.random.fold_in(own, position), (shards_of,), jnp.float32, smallest / len(shards), high / len(shards)))
        gain = gain * jnp.repeat(steps, dims[position] // shards_of).reshape([-1 if axis == position else 1 for axis in range(len(dims))])
    return gain


def split_up(number_of, total, reach, skew):
    portions = [(1 << 20) // math.isqrt(grade ** skew) + 1 for grade in range(2, number_of + 1)]
    spare, holding = total - reach - (number_of - 1), [1] * (number_of - 1)
    while spare > 0:
        candidates = [i for i in range(number_of - 1) if holding[i] < reach]
        pool, left = sum([portions[i] for i in candidates]), spare
        for i in candidates:
            more = min(reach - holding[i], max(1, left * portions[i] // pool), spare)
            holding[i] = holding[i] + more
            spare = spare - more
    return np.array([reach] + holding)


def ragged(stream_key, count, total, most, lean):
    if count == 2:
        one = jax.random.randint(stream_key, (), max(1, total - most), min(most, total - 1) + 1)
        return jnp.stack([one, total - one])
    lengths = jnp.asarray(split_up(count, total, most, lean), jnp.int32)
    pairs = (count - 1) // 2
    giver, sink = lengths[1:1 + 2 * pairs:2], lengths[2:2 + 2 * pairs:2]
    room = jnp.minimum(giver - 1, most - sink)
    shifted = jax.random.randint(jax.random.fold_in(stream_key, 1), (pairs,), 0, 1 << 20) % (room + 1)
    lengths = lengths.at[1:1 + 2 * pairs:2].set(giver - shifted).at[2:2 + 2 * pairs:2].set(sink + shifted)
    return lengths[jax.random.permutation(jax.random.fold_in(stream_key, 2), count)]


def gaussian(rng, shape, scale, bound, pieces=(), held_as=jnp.bfloat16):
    values = scale * jax.random.normal(rng, shape, jnp.float32)
    if pieces:
        values = values * levels(rng, shape, pieces, -0.22, 0.18)
    return jnp.clip(values, -bound, bound).astype(held_as)


def gaussian_with(rng, extent, deviation, limit, pieces, heavy, kind=jnp.bfloat16):
    result = deviation * jax.random.normal(rng, extent, jnp.float32)
    if pieces:
        result = result * levels(rng, extent, pieces, -0.22, 0.18)
    return jnp.clip(spiked(result, jax.random.fold_in(rng, 3), *heavy), -limit, limit).astype(kind)


def setup_inputs(seed: int = 0) -> dict:
    seeds = jax.random.split(jax.random.key(seed), 9)
    return {
        "inputs": gaussian_with(seeds[0], (SECTIONS, TOKENS, D), 1.0, 16.0, ((0, 4), (1, 64)), (1, 2, 64, 4.0)),
        "q_raw": gaussian(seeds[1], (SECTIONS, TOKENS, QHEADS * HEAD), 1.0, 6.0, ((0, 4), (1, 64))),
        "grad_out": gaussian(seeds[2], (SECTIONS, TOKENS, QHEADS * HEAD), 0.5, 6.0, ((0, 4), (1, 64))),
        "segments": jax.vmap(lambda own: jnp.searchsorted(jnp.cumsum(ragged(own, DOCS, TOKENS, DOC_MOST, 2)), jnp.arange(TOKENS), side="right"))(jax.random.split(seeds[3], SECTIONS)).reshape((SECTIONS, TOKENS)).astype(jnp.int32),
        "w_key": gaussian(seeds[4], (SECTIONS, D, KVW), D ** -0.5, 0.09375, ((0, 4), (1, 64))),
        "w_value": gaussian(seeds[5], (SECTIONS, D, KVW), D ** -0.5, 0.09375, ((0, 4), (1, 64))),
        "q_gain": jnp.clip(1.0 + 0.18 * jax.random.normal(seeds[6], (SECTIONS, HEAD), jnp.float32), 0.1, 1.9),
        "k_gain": jnp.clip(1.0 + 0.18 * jax.random.normal(seeds[7], (SECTIONS, HEAD), jnp.float32), 0.1, 1.9),
    }


epsilon = 1e-06
theta_base = 1000000.0

def rope_tables(positions):
    half_width = HEAD // 2
    frequency = jnp.exp(jnp.arange(half_width, dtype=jnp.float32) * (-2.0 * jnp.log(jnp.float32(theta_base)) / HEAD))
    angles = positions.astype(jnp.float32)[:, None] * frequency[None, :]
    return (jnp.cos(angles), jnp.sin(angles))

def rotate(values, cosine, sine_table):
    half_width = values.shape[-1] // 2
    front_half = values[..., :half_width]
    back_half = values[..., half_width:]
    cos_b = cosine[:, None, :]
    sin_b = sine_table[:, None, :]
    return jnp.concatenate([front_half * cos_b - back_half * sin_b, back_half * cos_b + front_half * sin_b], -1)

def unrotate(upstream, cosine, sine_table):
    half_width = upstream.shape[-1] // 2
    front_half = upstream[..., :half_width]
    back_half = upstream[..., half_width:]
    cos_b = cosine[:, None, :]
    sin_b = sine_table[:, None, :]
    return jnp.concatenate([front_half * cos_b + back_half * sin_b, back_half * cos_b - front_half * sin_b], -1)

def normalize(values, gain_row):
    inverse = lax.rsqrt(lax.optimization_barrier(jnp.mean(values * values, -1, keepdims=True)) + epsilon)
    return (values * inverse * gain_row, inverse)

def normalize_back(values, inverse, gain_row, upstream):
    scaled = upstream * gain_row
    cubed = inverse * inverse * inverse
    return inverse * scaled - values * cubed * lax.optimization_barrier(jnp.mean(values * scaled, -1, keepdims=True))

def section_backward(inputs, q_raw, grad_out, segments, w_key, w_value, q_gain, k_gain):
    length_all = inputs.shape[0]
    kv_width = w_key.shape[1]
    kv_heads = kv_width // HEAD
    q_heads = q_raw.shape[1] // HEAD
    group = q_heads // kv_heads
    score_scale = HEAD ** (-0.5)
    front_pad = WINDOW // TOK_DEV * TOK_DEV
    key_raw = jnp.dot(inputs, w_key, preferred_element_type=jnp.float32).astype(jnp.bfloat16)
    value_all = jnp.dot(inputs, w_value, preferred_element_type=jnp.float32).astype(jnp.bfloat16).reshape(length_all, kv_heads, HEAD)
    positions = jnp.arange(length_all, dtype=jnp.int32)
    cosine, sine_table = rope_tables(positions)
    query_in = q_raw.astype(jnp.float32).reshape(length_all, q_heads, HEAD)
    query_norm, query_inv = normalize(query_in, q_gain)
    query_rot = rotate(query_norm, cosine, sine_table).astype(jnp.bfloat16)
    key_in = key_raw.astype(jnp.float32).reshape(length_all, kv_heads, HEAD)
    key_norm, key_inv = normalize(key_in, k_gain)
    key_rot = rotate(key_norm, cosine, sine_table).astype(jnp.bfloat16)
    key_pad = jnp.concatenate([jnp.zeros((front_pad, kv_heads, HEAD), jnp.bfloat16), key_rot], 0)
    value_pad = jnp.concatenate([jnp.zeros((front_pad, kv_heads, HEAD), jnp.bfloat16), value_all], 0)
    seg_pad = jnp.concatenate([jnp.full((front_pad,), -1, jnp.int32), segments.astype(jnp.int32)], 0)
    out_grad = grad_out.reshape(length_all, kv_heads, group, HEAD)
    block_count = length_all // TOK_DEV

    def rounded(part):
        return lax.optimization_barrier(part.astype(jnp.bfloat16)).astype(jnp.float32)

    def one_block(carry, block_id):
        key_accum, value_accum = carry
        begin = (block_id * TOK_DEV).astype(jnp.int32)
        query_tile = lax.dynamic_slice_in_dim(query_rot, begin, TOK_DEV, 0).reshape(TOK_DEV, kv_heads, group, HEAD).astype(jnp.float32)
        key_tile = lax.dynamic_slice_in_dim(key_pad, begin, front_pad + TOK_DEV, 0).astype(jnp.float32)
        value_tile = lax.dynamic_slice_in_dim(value_pad, begin, front_pad + TOK_DEV, 0).astype(jnp.float32)
        grad_tile = lax.dynamic_slice_in_dim(out_grad, begin, TOK_DEV, 0).astype(jnp.float32)
        query_pos = begin + jnp.arange(TOK_DEV, dtype=jnp.int32)
        key_pos = begin - front_pad + jnp.arange(front_pad + TOK_DEV, dtype=jnp.int32)
        seg_query = lax.dynamic_slice_in_dim(segments.astype(jnp.int32), begin, TOK_DEV, 0)
        seg_key = lax.dynamic_slice_in_dim(seg_pad, begin, front_pad + TOK_DEV, 0)
        offset = query_pos[:, None] - key_pos[None, :]
        allowed = (offset >= 0) & (offset < WINDOW) & (key_pos >= 0)[None, :] & (seg_query[:, None] == seg_key[None, :])
        scores = jnp.einsum('qgrd,kgd->grqk', query_tile, key_tile) * score_scale
        exp_score = jnp.where(allowed, jnp.exp(scores), 0.0)
        row_total = lax.optimization_barrier(jnp.sum(exp_score, -1, keepdims=True))
        prob_tile = (exp_score / row_total).astype(jnp.bfloat16).astype(jnp.float32)
        attn_out = jnp.einsum('grqk,kgd->qgrd', prob_tile, value_tile)
        row_delta = lax.optimization_barrier(jnp.sum(grad_tile * attn_out, -1)).transpose(1, 2, 0)[..., None]
        prob_grad = jnp.einsum('qgrd,kgd->grqk', grad_tile, value_tile)
        score_grad = (prob_tile * (prob_grad - row_delta)).astype(jnp.bfloat16).astype(jnp.float32)
        value_part = jnp.einsum('grqk,qgrd->kgd', prob_tile, grad_tile)
        key_part = jnp.einsum('grqk,qgrd->kgd', score_grad, query_tile) * score_scale
        query_part = jnp.einsum('grqk,kgd->qgrd', score_grad, key_tile) * score_scale
        key_part = jnp.concatenate([rounded(key_part[:front_pad]), key_part[front_pad:]], 0)
        value_part = jnp.concatenate([rounded(value_part[:front_pad]), value_part[front_pad:]], 0)
        key_accum = lax.dynamic_update_slice_in_dim(key_accum, lax.dynamic_slice_in_dim(key_accum, begin, front_pad + TOK_DEV, 0) + key_part, begin, 0)
        value_accum = lax.dynamic_update_slice_in_dim(value_accum, lax.dynamic_slice_in_dim(value_accum, begin, front_pad + TOK_DEV, 0) + value_part, begin, 0)
        return ((key_accum, value_accum), query_part.reshape(TOK_DEV, q_heads, HEAD))
    start_accum = jnp.zeros((front_pad + length_all, kv_heads, HEAD), jnp.float32)
    (key_accum, value_accum), query_parts = lax.scan(one_block, (start_accum, start_accum), jnp.arange(block_count, dtype=jnp.int32))
    query_rot_grad = query_parts.reshape(length_all, q_heads, HEAD)
    key_rot_grad = key_accum[front_pad:]
    value_grad = value_accum[front_pad:]
    query_grad = normalize_back(query_in, query_inv, q_gain, unrotate(query_rot_grad, cosine, sine_table))
    query_grad = query_grad.reshape(length_all, q_heads * HEAD).astype(jnp.bfloat16)
    key_back = normalize_back(key_in, key_inv, k_gain, unrotate(key_rot_grad, cosine, sine_table))
    key_back = key_back.reshape(length_all, kv_width).astype(jnp.bfloat16)
    value_back = value_grad.reshape(length_all, kv_width).astype(jnp.bfloat16)
    key_weight_grad = jnp.dot(inputs.T, key_back, preferred_element_type=jnp.float32)
    value_weight_grad = jnp.dot(inputs.T, value_back, preferred_element_type=jnp.float32)
    input_grad = jnp.dot(key_back, w_key.T, preferred_element_type=jnp.float32) + jnp.dot(value_back, w_value.T, preferred_element_type=jnp.float32)
    return (query_grad, key_weight_grad, value_weight_grad, input_grad.astype(jnp.bfloat16))

def reference(inputs, q_raw, grad_out, segments, w_key, w_value, q_gain, k_gain):
    results = []
    for section in range(SECTIONS):
        results.append(section_backward(inputs[section], q_raw[section], grad_out[section], segments[section], w_key[section], w_value[section], q_gain[section], k_gain[section]))
    query_grad = jnp.stack([item[0] for item in results])
    key_weight_grad = jnp.stack([item[1] for item in results])
    value_weight_grad = jnp.stack([item[2] for item in results])
    input_grads = jnp.stack([item[3] for item in results])
    section_grad = jnp.roll(input_grads, -1, axis=0)
    return (query_grad, key_weight_grad, value_weight_grad, section_grad)
```

```python
import jax
import jax.numpy as jnp
from jax import lax
import functools

from jax.sharding import Mesh, NamedSharding, PartitionSpec as P

HEAD = 128
WINDOW = 768


epsilon = 1e-06
theta_base = 1000000.0


def axis_count(axis):
    names = axis if isinstance(axis, tuple) else (axis,)
    count = 1
    for name in names:
        count *= lax.axis_size(name)
    return count


def passed_along(block, axis, distance):
    devices = range(axis_count(axis))
    route = [(i - distance, i) for i in devices if i - distance in devices]
    return lax.ppermute(block, axis, route)


def shifted(shard, axis, by):
    devices = axis_count(axis)
    return lax.ppermute(shard, axis, [(i, (i + by) % devices) for i in range(devices)])


def rope_tables(positions):
    half_width = HEAD // 2
    frequency = jnp.exp(
        jnp.arange(half_width, dtype=jnp.float32) * (-2.0 * jnp.log(jnp.float32(theta_base)) / HEAD)
    )
    angles = positions.astype(jnp.float32)[:, None] * frequency[None, :]
    return (jnp.cos(angles), jnp.sin(angles))


def rotate(values, cosine, sine_table):
    half_width = values.shape[-1] // 2
    front_half = values[..., :half_width]
    back_half = values[..., half_width:]
    cos_b = cosine[:, None, :]
    sin_b = sine_table[:, None, :]
    return jnp.concatenate(
        [front_half * cos_b - back_half * sin_b, back_half * cos_b + front_half * sin_b], -1
    )


def unrotate(upstream, cosine, sine_table):
    half_width = upstream.shape[-1] // 2
    front_half = upstream[..., :half_width]
    back_half = upstream[..., half_width:]
    cos_b = cosine[:, None, :]
    sin_b = sine_table[:, None, :]
    return jnp.concatenate(
        [front_half * cos_b + back_half * sin_b, back_half * cos_b - front_half * sin_b], -1
    )


def normalize(values, gain_row):
    inverse = lax.rsqrt(jnp.mean(values * values, -1, keepdims=True) + epsilon)
    return (values * inverse * gain_row, inverse)


def normalize_back(values, inverse, gain_row, upstream):
    scaled = upstream * gain_row
    cubed = inverse * inverse * inverse
    return inverse * scaled - values * cubed * jnp.mean(values * scaled, -1, keepdims=True)


def guarded(tile_work, operands):
    return tile_work(*operands)


def local(inputs, q_raw, grad_out, segments, w_key, w_value, q_gain, k_gain, row_parts, col_parts):
    tokens_here = inputs[0]
    tok_rows = tokens_here.shape[0]
    kv_width = w_key.shape[2]
    kv_heads = kv_width // HEAD
    q_heads = q_raw.shape[2] // HEAD
    group = q_heads // kv_heads
    score_scale = HEAD ** (-0.5)
    reach_blocks = WINDOW // tok_rows
    col_index = lax.axis_index("cz")
    ctx_index = lax.axis_index("cb") * col_parts + col_index
    both_rows = jnp.concatenate([w_key[0], w_value[0]], 1)
    weight_slice = lax.all_gather(both_rows, "cz", axis=0, tiled=True)
    inputs_slice = lax.all_to_all(tokens_here, "cb", 1, 0, tiled=True)
    projected = lax.psum_scatter(
        jnp.dot(inputs_slice, weight_slice, preferred_element_type=jnp.float32),
        "cb",
        scatter_dimension=0,
        tiled=True,
    )
    key_raw = projected[:, :kv_width].astype(jnp.bfloat16)
    value_own = projected[:, kv_width:].astype(jnp.bfloat16).reshape(tok_rows, kv_heads, HEAD)
    local_pos = jnp.arange(tok_rows, dtype=jnp.int32)
    positions = ctx_index * tok_rows + local_pos
    cosine, sine_table = rope_tables(positions)
    query_in = q_raw[0].astype(jnp.float32).reshape(tok_rows, q_heads, HEAD)
    query_norm, query_inv = normalize(query_in, q_gain[0])
    query_rot = rotate(query_norm, cosine, sine_table).astype(jnp.bfloat16)
    key_in = key_raw.astype(jnp.float32).reshape(tok_rows, kv_heads, HEAD)
    key_norm, key_inv = normalize(key_in, k_gain[0])
    key_rot = rotate(key_norm, cosine, sine_table).astype(jnp.bfloat16)
    own_pair = jnp.stack([key_rot, value_own])
    key_blocks = [own_pair]
    for distance in range(1, reach_blocks + 1):
        key_blocks.append(passed_along(own_pair, CTX, distance))
    seg_all = segments[0]
    seg_query = lax.dynamic_slice_in_dim(seg_all, ctx_index * tok_rows, tok_rows)
    allowed_list = []
    for distance in range(reach_blocks + 1):
        key_pos = (ctx_index - distance) * tok_rows + local_pos
        seg_key = lax.dynamic_slice_in_dim(
            seg_all, jnp.maximum(ctx_index - distance, 0) * tok_rows, tok_rows
        )
        offset = positions[:, None] - key_pos[None, :]
        allowed = (
            (offset >= 0)
            & (offset < WINDOW)
            & (key_pos >= 0)[None, :]
            & (seg_query[:, None] == seg_key[None, :])
        )
        allowed_list.append(allowed)
    q_group = query_rot.reshape(tok_rows, kv_heads, group, HEAD)
    out_grad = grad_out[0].reshape(tok_rows, kv_heads, group, HEAD)

    def exp_block(key_pair, allowed):
        scores = (
            jnp.einsum("qgrd,kgd->grqk", q_group, key_pair[0], preferred_element_type=jnp.float32)
            * score_scale
        )
        return jnp.where(allowed, jnp.exp(scores), 0.0)

    def total_block(key_pair, allowed):
        return jnp.sum(exp_block(key_pair, allowed), -1)

    zero_total = jnp.zeros((kv_heads, group, tok_rows), jnp.float32)
    row_total = zero_total
    for distance in range(reach_blocks + 1):
        row_total = row_total + guarded(total_block, (key_blocks[distance], allowed_list[distance]))

    def prob_block(key_pair, allowed):
        prob_tile = (exp_block(key_pair, allowed) / row_total[..., None]).astype(jnp.bfloat16)
        out_tile = jnp.einsum(
            "grqk,kgd->qgrd", prob_tile, key_pair[1], preferred_element_type=jnp.float32
        )
        return (prob_tile, out_tile)

    zero_query = jnp.zeros((tok_rows, kv_heads, group, HEAD), jnp.float32)
    prob_list = []
    attn_out = zero_query
    for distance in range(reach_blocks + 1):
        prob_tile, out_tile = guarded(prob_block, (key_blocks[distance], allowed_list[distance]))
        prob_list.append(prob_tile)
        attn_out = attn_out + out_tile
    row_delta = jnp.sum(out_grad.astype(jnp.float32) * attn_out, -1).transpose(1, 2, 0)[..., None]

    def grad_block(key_pair, prob_tile):
        prob_grad = jnp.einsum(
            "qgrd,kgd->grqk", out_grad, key_pair[1], preferred_element_type=jnp.float32
        )
        score_grad = (prob_tile.astype(jnp.float32) * (prob_grad - row_delta)).astype(jnp.bfloat16)
        value_grad = jnp.einsum(
            "grqk,qgrd->kgd", prob_tile, out_grad, preferred_element_type=jnp.float32
        )
        key_grad = (
            jnp.einsum("grqk,qgrd->kgd", score_grad, q_group, preferred_element_type=jnp.float32)
            * score_scale
        )
        query_part = (
            jnp.einsum(
                "grqk,kgd->qgrd", score_grad, key_pair[0], preferred_element_type=jnp.float32
            )
            * score_scale
        )
        return (query_part, jnp.stack([key_grad, value_grad]))

    zero_pair = jnp.zeros((2, tok_rows, kv_heads, HEAD), jnp.float32)
    query_rot_grad = zero_query
    kv_total = zero_pair
    for distance in range(reach_blocks + 1):
        query_part, kv_part = guarded(grad_block, (key_blocks[distance], prob_list[distance]))
        query_rot_grad = query_rot_grad + query_part
        if distance == 0:
            kv_total = kv_part
        else:
            returned = passed_along(kv_part.astype(jnp.bfloat16), CTX, -distance)
            kv_total = kv_total + returned.astype(jnp.float32)
    query_grad = normalize_back(
        query_in,
        query_inv,
        q_gain[0],
        unrotate(query_rot_grad.reshape(tok_rows, q_heads, HEAD), cosine, sine_table),
    )
    query_grad = query_grad.reshape(tok_rows, q_heads * HEAD).astype(jnp.bfloat16)
    key_back = normalize_back(key_in, key_inv, k_gain[0], unrotate(kv_total[0], cosine, sine_table))
    key_back = key_back.reshape(tok_rows, kv_width).astype(jnp.bfloat16)
    value_back = kv_total[1].reshape(tok_rows, kv_width).astype(jnp.bfloat16)
    both_back = jnp.concatenate([key_back, value_back], 1)
    group_back = lax.all_gather(both_back, "cb", axis=0, tiled=True)
    grad_rows = lax.psum_scatter(
        lax.dot_general(
            inputs_slice, group_back, (((0,), (0,)), ((), ())), preferred_element_type=jnp.float32
        ),
        "cz",
        scatter_dimension=0,
        tiled=True,
    )
    slice_grad = lax.dot_general(
        group_back, weight_slice, (((1,), (1,)), ((), ())), preferred_element_type=jnp.float32
    ).astype(jnp.bfloat16)
    input_grad = lax.all_to_all(slice_grad, "cb", 0, 1, tiled=True)
    passed = shifted(input_grad, "pipe", -1)
    return (
        query_grad[None],
        grad_rows[:, :kv_width][None],
        grad_rows[:, kv_width:][None],
        passed[None],
    )


CTX = ("cb", "cz")


def solution(mesh):
    col_parts = 8
    row_parts = mesh.shape["ctx"] // col_parts
    grid = mesh.devices.reshape(row_parts, col_parts, mesh.shape["pipe"])
    split_mesh = Mesh(grid, ("cb", "cz", "pipe"))
    rows = P("pipe", CTX, None)
    inner = jax.shard_map(
        functools.partial(local, row_parts=row_parts, col_parts=col_parts),
        mesh=split_mesh,
        in_specs=(rows, rows, rows, P("pipe", None), rows, rows, P("pipe", None), P("pipe", None)),
        out_specs=(rows, rows, rows, rows),
        check_vma=False,
    )
    placed = NamedSharding(mesh, P("pipe", "ctx", None))

    def run(*args):
        return tuple(lax.with_sharding_constraint(out, placed) for out in inner(*args))

    return run
```

```python
import jax
import jax.numpy as jnp
from jax import lax
import functools

from jax.sharding import Mesh, NamedSharding, PartitionSpec as P

HEAD = 128
WINDOW = 768


epsilon = 1e-06
theta_base = 1000000.0


def axis_count(axis):
    names = axis if isinstance(axis, tuple) else (axis,)
    count = 1
    for name in names:
        count *= lax.axis_size(name)
    return count


def passed_along(block, axis, distance):
    devices = range(axis_count(axis))
    route = [(i - distance, i) for i in devices if i - distance in devices]
    return lax.ppermute(block, axis, route)


def shifted(shard, axis, by):
    devices = axis_count(axis)
    return lax.ppermute(shard, axis, [(i, (i + by) % devices) for i in range(devices)])


def rope_tables(positions):
    half_width = HEAD // 2
    frequency = jnp.exp(
        jnp.arange(half_width, dtype=jnp.float32) * (-2.0 * jnp.log(jnp.float32(theta_base)) / HEAD)
    )
    angles = positions.astype(jnp.float32)[:, None] * frequency[None, :]
    return (jnp.cos(angles), jnp.sin(angles))


def rotate(values, cosine, sine_table):
    half_width = values.shape[-1] // 2
    front_half = values[..., :half_width]
    back_half = values[..., half_width:]
    cos_b = cosine[:, None, :]
    sin_b = sine_table[:, None, :]
    return jnp.concatenate(
        [front_half * cos_b - back_half * sin_b, back_half * cos_b + front_half * sin_b], -1
    )


def unrotate(upstream, cosine, sine_table):
    half_width = upstream.shape[-1] // 2
    front_half = upstream[..., :half_width]
    back_half = upstream[..., half_width:]
    cos_b = cosine[:, None, :]
    sin_b = sine_table[:, None, :]
    return jnp.concatenate(
        [front_half * cos_b + back_half * sin_b, back_half * cos_b - front_half * sin_b], -1
    )


def normalize(values, gain_row):
    inverse = lax.rsqrt(jnp.mean(values * values, -1, keepdims=True) + epsilon)
    return (values * inverse * gain_row, inverse)


def normalize_back(values, inverse, gain_row, upstream):
    scaled = upstream * gain_row
    cubed = inverse * inverse * inverse
    return inverse * scaled - values * cubed * jnp.mean(values * scaled, -1, keepdims=True)


def gathered(block, axis, parts):
    copies = jnp.broadcast_to(block[None], (parts,) + block.shape)
    received = lax.all_to_all(copies, axis, 0, 0, tiled=True)
    return received.reshape((parts * block.shape[0],) + block.shape[1:])


def summed_over(partial, axis, parts, sent_as):
    pieces = partial.astype(sent_as).reshape((parts, partial.shape[0] // parts) + partial.shape[1:])
    received = lax.all_to_all(pieces, axis, 0, 0, tiled=True)
    return jnp.sum(received.astype(jnp.float32), 0)


def guarded(tile_work, operands):
    return tile_work(*operands)


def local(inputs, q_raw, grad_out, segments, w_key, w_value, q_gain, k_gain, row_parts, col_parts):
    tokens_here = inputs[0]
    tok_rows = tokens_here.shape[0]
    kv_width = w_key.shape[2]
    kv_heads = kv_width // HEAD
    q_heads = q_raw.shape[2] // HEAD
    group = q_heads // kv_heads
    score_scale = HEAD ** (-0.5)
    reach_blocks = WINDOW // tok_rows
    col_index = lax.axis_index("cz")
    ctx_index = lax.axis_index("cb") * col_parts + col_index
    both_rows = jnp.concatenate([w_key[0], w_value[0]], 1)
    weight_slice = gathered(both_rows, "cz", col_parts)
    inputs_slice = lax.all_to_all(tokens_here, "cb", 1, 0, tiled=True)
    projected = summed_over(
        jnp.dot(inputs_slice, weight_slice, preferred_element_type=jnp.float32),
        "cb",
        row_parts,
        jnp.bfloat16,
    )
    key_raw = projected[:, :kv_width].astype(jnp.bfloat16)
    value_own = projected[:, kv_width:].astype(jnp.bfloat16).reshape(tok_rows, kv_heads, HEAD)
    local_pos = jnp.arange(tok_rows, dtype=jnp.int32)
    positions = ctx_index * tok_rows + local_pos
    cosine, sine_table = rope_tables(positions)
    query_in = q_raw[0].astype(jnp.float32).reshape(tok_rows, q_heads, HEAD)
    query_norm, query_inv = normalize(query_in, q_gain[0])
    query_rot = rotate(query_norm, cosine, sine_table).astype(jnp.bfloat16)
    key_in = key_raw.astype(jnp.float32).reshape(tok_rows, kv_heads, HEAD)
    key_norm, key_inv = normalize(key_in, k_gain[0])
    key_rot = rotate(key_norm, cosine, sine_table).astype(jnp.bfloat16)
    own_pair = jnp.stack([key_rot, value_own])
    key_blocks = [own_pair]
    for distance in range(1, reach_blocks + 1):
        key_blocks.append(passed_along(own_pair, CTX, distance))
    seg_all = segments[0]
    seg_query = lax.dynamic_slice_in_dim(seg_all, ctx_index * tok_rows, tok_rows)
    allowed_list = []
    for distance in range(reach_blocks + 1):
        key_pos = (ctx_index - distance) * tok_rows + local_pos
        seg_key = lax.dynamic_slice_in_dim(
            seg_all, jnp.maximum(ctx_index - distance, 0) * tok_rows, tok_rows
        )
        offset = positions[:, None] - key_pos[None, :]
        allowed = (
            (offset >= 0)
            & (offset < WINDOW)
            & (key_pos >= 0)[None, :]
            & (seg_query[:, None] == seg_key[None, :])
        )
        allowed_list.append(allowed)
    q_group = query_rot.reshape(tok_rows, kv_heads, group, HEAD)
    out_grad = grad_out[0].reshape(tok_rows, kv_heads, group, HEAD)

    def exp_block(key_pair, allowed):
        scores = (
            jnp.einsum("qgrd,kgd->grqk", q_group, key_pair[0], preferred_element_type=jnp.float32)
            * score_scale
        )
        return jnp.where(allowed, jnp.exp(scores), 0.0)

    def total_block(key_pair, allowed):
        return jnp.sum(exp_block(key_pair, allowed), -1)

    zero_total = jnp.zeros((kv_heads, group, tok_rows), jnp.float32)
    row_total = zero_total
    for distance in range(reach_blocks + 1):
        row_total = row_total + guarded(total_block, (key_blocks[distance], allowed_list[distance]))

    def prob_block(key_pair, allowed):
        prob_tile = (exp_block(key_pair, allowed) / row_total[..., None]).astype(jnp.bfloat16)
        out_tile = jnp.einsum(
            "grqk,kgd->qgrd", prob_tile, key_pair[1], preferred_element_type=jnp.float32
        )
        return (prob_tile, out_tile)

    zero_query = jnp.zeros((tok_rows, kv_heads, group, HEAD), jnp.float32)
    prob_list = []
    attn_out = zero_query
    for distance in range(reach_blocks + 1):
        prob_tile, out_tile = guarded(prob_block, (key_blocks[distance], allowed_list[distance]))
        prob_list.append(prob_tile)
        attn_out = attn_out + out_tile
    row_delta = jnp.sum(out_grad.astype(jnp.float32) * attn_out, -1).transpose(1, 2, 0)[..., None]

    def grad_block(key_pair, prob_tile):
        prob_grad = jnp.einsum(
            "qgrd,kgd->grqk", out_grad, key_pair[1], preferred_element_type=jnp.float32
        )
        score_grad = (prob_tile.astype(jnp.float32) * (prob_grad - row_delta)).astype(jnp.bfloat16)
        value_grad = jnp.einsum(
            "grqk,qgrd->kgd", prob_tile, out_grad, preferred_element_type=jnp.float32
        )
        key_grad = (
            jnp.einsum("grqk,qgrd->kgd", score_grad, q_group, preferred_element_type=jnp.float32)
            * score_scale
        )
        query_part = (
            jnp.einsum(
                "grqk,kgd->qgrd", score_grad, key_pair[0], preferred_element_type=jnp.float32
            )
            * score_scale
        )
        return (query_part, jnp.stack([key_grad, value_grad]))

    zero_pair = jnp.zeros((2, tok_rows, kv_heads, HEAD), jnp.float32)
    query_rot_grad = zero_query
    kv_total = zero_pair
    for distance in range(reach_blocks + 1):
        query_part, kv_part = guarded(grad_block, (key_blocks[distance], prob_list[distance]))
        query_rot_grad = query_rot_grad + query_part
        if distance == 0:
            kv_total = kv_part
        else:
            returned = passed_along(kv_part.astype(jnp.bfloat16), CTX, -distance)
            kv_total = kv_total + returned.astype(jnp.float32)
    query_grad = normalize_back(
        query_in,
        query_inv,
        q_gain[0],
        unrotate(query_rot_grad.reshape(tok_rows, q_heads, HEAD), cosine, sine_table),
    )
    query_grad = query_grad.reshape(tok_rows, q_heads * HEAD).astype(jnp.bfloat16)
    key_back = normalize_back(key_in, key_inv, k_gain[0], unrotate(kv_total[0], cosine, sine_table))
    key_back = key_back.reshape(tok_rows, kv_width).astype(jnp.bfloat16)
    value_back = kv_total[1].reshape(tok_rows, kv_width).astype(jnp.bfloat16)
    both_back = jnp.concatenate([key_back, value_back], 1)
    group_back = gathered(both_back, "cb", row_parts)
    grad_rows = summed_over(
        lax.dot_general(
            inputs_slice, group_back, (((0,), (0,)), ((), ())), preferred_element_type=jnp.float32
        ),
        "cz",
        col_parts,
        jnp.float32,
    )
    slice_grad = lax.dot_general(
        group_back, weight_slice, (((1,), (1,)), ((), ())), preferred_element_type=jnp.float32
    ).astype(jnp.bfloat16)
    input_grad = lax.all_to_all(slice_grad, "cb", 0, 1, tiled=True)
    passed = shifted(input_grad, "pipe", -1)
    return (
        query_grad[None],
        grad_rows[:, :kv_width][None],
        grad_rows[:, kv_width:][None],
        passed[None],
    )


CTX = ("cb", "cz")


def solution(mesh):
    col_parts = 8
    row_parts = mesh.shape["ctx"] // col_parts
    grid = mesh.devices.reshape(row_parts, col_parts, mesh.shape["pipe"])
    split_mesh = Mesh(grid, ("cb", "cz", "pipe"))
    rows = P("pipe", CTX, None)
    inner = jax.shard_map(
        functools.partial(local, row_parts=row_parts, col_parts=col_parts),
        mesh=split_mesh,
        in_specs=(rows, rows, rows, P("pipe", None), rows, rows, P("pipe", None), P("pipe", None)),
        out_specs=(rows, rows, rows, rows),
        check_vma=False,
    )
    placed = NamedSharding(mesh, P("pipe", "ctx", None))

    def run(*args):
        return tuple(lax.with_sharding_constraint(out, placed) for out in inner(*args))

    return run
```

```python
import jax
import jax.numpy as jnp
from jax import lax
import functools

from jax.sharding import Mesh, NamedSharding, PartitionSpec as P

HEAD = 128
WINDOW = 768


epsilon = 1e-06
theta_base = 1000000.0


def axis_count(axis):
    names = axis if isinstance(axis, tuple) else (axis,)
    count = 1
    for name in names:
        count *= lax.axis_size(name)
    return count


def passed_along(block, axis, distance):
    devices = range(axis_count(axis))
    route = [(i - distance, i) for i in devices if i - distance in devices]
    return lax.ppermute(block, axis, route)


def shifted(shard, axis, by):
    devices = axis_count(axis)
    return lax.ppermute(shard, axis, [(i, (i + by) % devices) for i in range(devices)])


def rope_tables(positions):
    half_width = HEAD // 2
    frequency = jnp.exp(
        jnp.arange(half_width, dtype=jnp.float32) * (-2.0 * jnp.log(jnp.float32(theta_base)) / HEAD)
    )
    angles = positions.astype(jnp.float32)[:, None] * frequency[None, :]
    return (jnp.cos(angles), jnp.sin(angles))


def rotate(values, cosine, sine_table):
    half_width = values.shape[-1] // 2
    front_half = values[..., :half_width]
    back_half = values[..., half_width:]
    cos_b = cosine[:, None, :]
    sin_b = sine_table[:, None, :]
    return jnp.concatenate(
        [front_half * cos_b - back_half * sin_b, back_half * cos_b + front_half * sin_b], -1
    )


def unrotate(upstream, cosine, sine_table):
    half_width = upstream.shape[-1] // 2
    front_half = upstream[..., :half_width]
    back_half = upstream[..., half_width:]
    cos_b = cosine[:, None, :]
    sin_b = sine_table[:, None, :]
    return jnp.concatenate(
        [front_half * cos_b + back_half * sin_b, back_half * cos_b - front_half * sin_b], -1
    )


def normalize(values, gain_row):
    inverse = lax.rsqrt(jnp.mean(values * values, -1, keepdims=True) + epsilon)
    return (values * inverse * gain_row, inverse)


def normalize_back(values, inverse, gain_row, upstream):
    scaled = upstream * gain_row
    cubed = inverse * inverse * inverse
    return inverse * scaled - values * cubed * jnp.mean(values * scaled, -1, keepdims=True)


def gathered(block, axis, parts):
    copies = jnp.broadcast_to(block[None], (parts,) + block.shape)
    received = lax.all_to_all(copies, axis, 0, 0, tiled=True)
    return received.reshape((parts * block.shape[0],) + block.shape[1:])


def summed_over(partial, axis, parts, sent_as):
    pieces = partial.astype(sent_as).reshape((parts, partial.shape[0] // parts) + partial.shape[1:])
    received = lax.all_to_all(pieces, axis, 0, 0, tiled=True)
    return jnp.sum(received.astype(jnp.float32), 0)


def guarded(tile_work, operands):
    return tile_work(*operands)


def local(inputs, q_raw, grad_out, segments, w_key, w_value, q_gain, k_gain, row_parts, col_parts):
    tokens_here = inputs[0]
    tok_rows = tokens_here.shape[0]
    kv_width = w_key.shape[2]
    kv_heads = kv_width // HEAD
    q_heads = q_raw.shape[2] // HEAD
    group = q_heads // kv_heads
    score_scale = HEAD ** (-0.5)
    reach_blocks = WINDOW // tok_rows
    col_index = lax.axis_index("cz")
    ctx_index = lax.axis_index("cb") * col_parts + col_index
    both_rows = jnp.concatenate([w_key[0], w_value[0]], 1)
    weight_slice = lax.all_gather(both_rows, "cz", axis=0, tiled=True)
    inputs_slice = lax.all_to_all(tokens_here, "cb", 1, 0, tiled=True)
    projected = summed_over(
        jnp.dot(inputs_slice, weight_slice, preferred_element_type=jnp.float32),
        "cb",
        row_parts,
        jnp.bfloat16,
    )
    key_raw = projected[:, :kv_width].astype(jnp.bfloat16)
    value_own = projected[:, kv_width:].astype(jnp.bfloat16).reshape(tok_rows, kv_heads, HEAD)
    local_pos = jnp.arange(tok_rows, dtype=jnp.int32)
    positions = ctx_index * tok_rows + local_pos
    cosine, sine_table = rope_tables(positions)
    query_in = q_raw[0].astype(jnp.float32).reshape(tok_rows, q_heads, HEAD)
    query_norm, query_inv = normalize(query_in, q_gain[0])
    query_rot = rotate(query_norm, cosine, sine_table).astype(jnp.bfloat16)
    key_in = key_raw.astype(jnp.float32).reshape(tok_rows, kv_heads, HEAD)
    key_norm, key_inv = normalize(key_in, k_gain[0])
    key_rot = rotate(key_norm, cosine, sine_table).astype(jnp.bfloat16)
    own_pair = jnp.stack([key_rot, value_own])
    key_blocks = [own_pair]
    for distance in range(1, reach_blocks + 1):
        key_blocks.append(passed_along(own_pair, CTX, distance))
    seg_all = segments[0]
    seg_query = lax.dynamic_slice_in_dim(seg_all, ctx_index * tok_rows, tok_rows)
    allowed_list = []
    for distance in range(reach_blocks + 1):
        key_pos = (ctx_index - distance) * tok_rows + local_pos
        seg_key = lax.dynamic_slice_in_dim(
            seg_all, jnp.maximum(ctx_index - distance, 0) * tok_rows, tok_rows
        )
        offset = positions[:, None] - key_pos[None, :]
        allowed = (
            (offset >= 0)
            & (offset < WINDOW)
            & (key_pos >= 0)[None, :]
            & (seg_query[:, None] == seg_key[None, :])
        )
        allowed_list.append(allowed)
    q_group = query_rot.reshape(tok_rows, kv_heads, group, HEAD)
    out_grad = grad_out[0].reshape(tok_rows, kv_heads, group, HEAD)

    def exp_block(key_pair, allowed):
        scores = (
            jnp.einsum("qgrd,kgd->grqk", q_group, key_pair[0], preferred_element_type=jnp.float32)
            * score_scale
        )
        return jnp.where(allowed, jnp.exp(scores), 0.0)

    def total_block(key_pair, allowed):
        return jnp.sum(exp_block(key_pair, allowed), -1)

    zero_total = jnp.zeros((kv_heads, group, tok_rows), jnp.float32)
    row_total = zero_total
    for distance in range(reach_blocks + 1):
        row_total = row_total + guarded(total_block, (key_blocks[distance], allowed_list[distance]))

    def prob_block(key_pair, allowed):
        prob_tile = (exp_block(key_pair, allowed) / row_total[..., None]).astype(jnp.bfloat16)
        out_tile = jnp.einsum(
            "grqk,kgd->qgrd", prob_tile, key_pair[1], preferred_element_type=jnp.float32
        )
        return (prob_tile, out_tile)

    zero_query = jnp.zeros((tok_rows, kv_heads, group, HEAD), jnp.float32)
    prob_list = []
    attn_out = zero_query
    for distance in range(reach_blocks + 1):
        prob_tile, out_tile = guarded(prob_block, (key_blocks[distance], allowed_list[distance]))
        prob_list.append(prob_tile)
        attn_out = attn_out + out_tile
    row_delta = jnp.sum(out_grad.astype(jnp.float32) * attn_out, -1).transpose(1, 2, 0)[..., None]

    def grad_block(key_pair, prob_tile):
        prob_grad = jnp.einsum(
            "qgrd,kgd->grqk", out_grad, key_pair[1], preferred_element_type=jnp.float32
        )
        score_grad = (prob_tile.astype(jnp.float32) * (prob_grad - row_delta)).astype(jnp.bfloat16)
        value_grad = jnp.einsum(
            "grqk,qgrd->kgd", prob_tile, out_grad, preferred_element_type=jnp.float32
        )
        key_grad = (
            jnp.einsum("grqk,qgrd->kgd", score_grad, q_group, preferred_element_type=jnp.float32)
            * score_scale
        )
        query_part = (
            jnp.einsum(
                "grqk,kgd->qgrd", score_grad, key_pair[0], preferred_element_type=jnp.float32
            )
            * score_scale
        )
        return (query_part, jnp.stack([key_grad, value_grad]))

    zero_pair = jnp.zeros((2, tok_rows, kv_heads, HEAD), jnp.float32)
    query_rot_grad = zero_query
    kv_total = zero_pair
    for distance in range(reach_blocks + 1):
        query_part, kv_part = guarded(grad_block, (key_blocks[distance], prob_list[distance]))
        query_rot_grad = query_rot_grad + query_part
        if distance == 0:
            kv_total = kv_part
        else:
            returned = passed_along(kv_part.astype(jnp.bfloat16), CTX, -distance)
            kv_total = kv_total + returned.astype(jnp.float32)
    query_grad = normalize_back(
        query_in,
        query_inv,
        q_gain[0],
        unrotate(query_rot_grad.reshape(tok_rows, q_heads, HEAD), cosine, sine_table),
    )
    query_grad = query_grad.reshape(tok_rows, q_heads * HEAD).astype(jnp.bfloat16)
    key_back = normalize_back(key_in, key_inv, k_gain[0], unrotate(kv_total[0], cosine, sine_table))
    key_back = key_back.reshape(tok_rows, kv_width).astype(jnp.bfloat16)
    value_back = kv_total[1].reshape(tok_rows, kv_width).astype(jnp.bfloat16)
    both_back = jnp.concatenate([key_back, value_back], 1)
    group_back = gathered(both_back, "cb", row_parts)
    grad_rows = lax.psum_scatter(
        lax.dot_general(
            inputs_slice, group_back, (((0,), (0,)), ((), ())), preferred_element_type=jnp.float32
        ),
        "cz",
        scatter_dimension=0,
        tiled=True,
    )
    slice_grad = lax.dot_general(
        group_back, weight_slice, (((1,), (1,)), ((), ())), preferred_element_type=jnp.float32
    ).astype(jnp.bfloat16)
    input_grad = lax.all_to_all(slice_grad, "cb", 0, 1, tiled=True)
    passed = shifted(input_grad, "pipe", -1)
    return (
        query_grad[None],
        grad_rows[:, :kv_width][None],
        grad_rows[:, kv_width:][None],
        passed[None],
    )


CTX = ("cb", "cz")


def solution(mesh):
    col_parts = 8
    row_parts = mesh.shape["ctx"] // col_parts
    grid = mesh.devices.reshape(row_parts, col_parts, mesh.shape["pipe"])
    split_mesh = Mesh(grid, ("cb", "cz", "pipe"))
    rows = P("pipe", CTX, None)
    inner = jax.shard_map(
        functools.partial(local, row_parts=row_parts, col_parts=col_parts),
        mesh=split_mesh,
        in_specs=(rows, rows, rows, P("pipe", None), rows, rows, P("pipe", None), P("pipe", None)),
        out_specs=(rows, rows, rows, rows),
        check_vma=False,
    )
    placed = NamedSharding(mesh, P("pipe", "ctx", None))

    def run(*args):
        return tuple(lax.with_sharding_constraint(out, placed) for out in inner(*args))

    return run
```

```python
import jax
import jax.numpy as jnp
from jax import lax
import functools

from jax.sharding import Mesh, NamedSharding, PartitionSpec as P

HEAD = 128
WINDOW = 768


epsilon = 1e-06
theta_base = 1000000.0


def axis_count(axis):
    names = axis if isinstance(axis, tuple) else (axis,)
    count = 1
    for name in names:
        count *= lax.axis_size(name)
    return count


def passed_along(block, axis, distance):
    devices = range(axis_count(axis))
    route = [(i - distance, i) for i in devices if i - distance in devices]
    return lax.ppermute(block, axis, route)


def shifted(shard, axis, by):
    devices = axis_count(axis)
    return lax.ppermute(shard, axis, [(i, (i + by) % devices) for i in range(devices)])


def rope_tables(positions):
    half_width = HEAD // 2
    frequency = jnp.exp(
        jnp.arange(half_width, dtype=jnp.float32) * (-2.0 * jnp.log(jnp.float32(theta_base)) / HEAD)
    )
    angles = positions.astype(jnp.float32)[:, None] * frequency[None, :]
    return (jnp.cos(angles), jnp.sin(angles))


def rotate(values, cosine, sine_table):
    half_width = values.shape[-1] // 2
    front_half = values[..., :half_width]
    back_half = values[..., half_width:]
    cos_b = cosine[:, None, :]
    sin_b = sine_table[:, None, :]
    return jnp.concatenate(
        [front_half * cos_b - back_half * sin_b, back_half * cos_b + front_half * sin_b], -1
    )


def unrotate(upstream, cosine, sine_table):
    half_width = upstream.shape[-1] // 2
    front_half = upstream[..., :half_width]
    back_half = upstream[..., half_width:]
    cos_b = cosine[:, None, :]
    sin_b = sine_table[:, None, :]
    return jnp.concatenate(
        [front_half * cos_b + back_half * sin_b, back_half * cos_b - front_half * sin_b], -1
    )


def normalize(values, gain_row):
    inverse = lax.rsqrt(jnp.mean(values * values, -1, keepdims=True) + epsilon)
    return (values * inverse * gain_row, inverse)


def normalize_back(values, inverse, gain_row, upstream):
    scaled = upstream * gain_row
    cubed = inverse * inverse * inverse
    return inverse * scaled - values * cubed * jnp.mean(values * scaled, -1, keepdims=True)


def gathered(block, axis, parts):
    copies = jnp.broadcast_to(block[None], (parts,) + block.shape)
    received = lax.all_to_all(copies, axis, 0, 0, tiled=True)
    return received.reshape((parts * block.shape[0],) + block.shape[1:])


def summed_over(partial, axis, parts, sent_as):
    pieces = partial.astype(sent_as).reshape((parts, partial.shape[0] // parts) + partial.shape[1:])
    received = lax.all_to_all(pieces, axis, 0, 0, tiled=True)
    return jnp.sum(received.astype(jnp.float32), 0)


def guarded(tile_work, operands):
    return tile_work(*operands)


def local(inputs, q_raw, grad_out, segments, w_key, w_value, q_gain, k_gain, row_parts, col_parts):
    tokens_here = inputs[0]
    tok_rows = tokens_here.shape[0]
    kv_width = w_key.shape[2]
    kv_heads = kv_width // HEAD
    q_heads = q_raw.shape[2] // HEAD
    group = q_heads // kv_heads
    score_scale = HEAD ** (-0.5)
    reach_blocks = WINDOW // tok_rows
    col_index = lax.axis_index("cz")
    ctx_index = lax.axis_index("cb") * col_parts + col_index
    both_rows = jnp.concatenate([w_key[0], w_value[0]], 1)
    weight_slice = lax.all_gather(both_rows, "cz", axis=0, tiled=True)
    inputs_slice = lax.all_to_all(tokens_here, "cb", 1, 0, tiled=True)
    projected = summed_over(
        jnp.dot(inputs_slice, weight_slice, preferred_element_type=jnp.float32),
        "cb",
        row_parts,
        jnp.bfloat16,
    )
    key_raw = projected[:, :kv_width].astype(jnp.bfloat16)
    value_own = projected[:, kv_width:].astype(jnp.bfloat16).reshape(tok_rows, kv_heads, HEAD)
    local_pos = jnp.arange(tok_rows, dtype=jnp.int32)
    positions = ctx_index * tok_rows + local_pos
    cosine, sine_table = rope_tables(positions)
    query_in = q_raw[0].astype(jnp.float32).reshape(tok_rows, q_heads, HEAD)
    query_norm, query_inv = normalize(query_in, q_gain[0])
    query_rot = rotate(query_norm, cosine, sine_table).astype(jnp.bfloat16)
    key_in = key_raw.astype(jnp.float32).reshape(tok_rows, kv_heads, HEAD)
    key_norm, key_inv = normalize(key_in, k_gain[0])
    key_rot = rotate(key_norm, cosine, sine_table).astype(jnp.bfloat16)
    own_pair = jnp.stack([key_rot, value_own])
    key_blocks = [own_pair]
    for distance in range(1, reach_blocks + 1):
        key_blocks.append(passed_along(own_pair, CTX, distance))
    seg_all = segments[0]
    seg_query = lax.dynamic_slice_in_dim(seg_all, ctx_index * tok_rows, tok_rows)
    allowed_list = []
    for distance in range(reach_blocks + 1):
        key_pos = (ctx_index - distance) * tok_rows + local_pos
        seg_key = lax.dynamic_slice_in_dim(
            seg_all, jnp.maximum(ctx_index - distance, 0) * tok_rows, tok_rows
        )
        offset = positions[:, None] - key_pos[None, :]
        allowed = (
            (offset >= 0)
            & (offset < WINDOW)
            & (key_pos >= 0)[None, :]
            & (seg_query[:, None] == seg_key[None, :])
        )
        allowed_list.append(allowed)
    q_group = query_rot.reshape(tok_rows, kv_heads, group, HEAD)
    out_grad = grad_out[0].reshape(tok_rows, kv_heads, group, HEAD)
    pairs = jnp.concatenate(key_blocks, 1)
    keys, values = pairs[0], pairs[1]
    allowed = jnp.concatenate(allowed_list, 1)
    scores = (
        jnp.einsum("qgrd,kgd->grqk", q_group, keys, preferred_element_type=jnp.float32)
        * score_scale
    )
    exp_score = jnp.where(allowed, jnp.exp(scores), 0.0)
    row_total = jnp.sum(exp_score, -1, keepdims=True)
    prob_tile = (exp_score / row_total).astype(jnp.bfloat16)
    attn_out = jnp.einsum(
        "grqk,kgd->qgrd", prob_tile, values, preferred_element_type=jnp.float32
    )
    row_delta = jnp.sum(out_grad.astype(jnp.float32) * attn_out, -1).transpose(1, 2, 0)[..., None]
    prob_grad = jnp.einsum(
        "qgrd,kgd->grqk", out_grad, values, preferred_element_type=jnp.float32
    )
    score_grad = (prob_tile.astype(jnp.float32) * (prob_grad - row_delta)).astype(jnp.bfloat16)
    value_grad = jnp.einsum(
        "grqk,qgrd->kgd", prob_tile, out_grad, preferred_element_type=jnp.float32
    )
    key_grad = (
        jnp.einsum("grqk,qgrd->kgd", score_grad, q_group, preferred_element_type=jnp.float32)
        * score_scale
    )
    query_rot_grad = (
        jnp.einsum("grqk,kgd->qgrd", score_grad, keys, preferred_element_type=jnp.float32)
        * score_scale
    )
    kv_parts = jnp.stack([key_grad, value_grad])
    kv_total = kv_parts[:, :tok_rows]
    for distance in range(1, reach_blocks + 1):
        kv_part = kv_parts[:, distance * tok_rows : (distance + 1) * tok_rows]
        returned = passed_along(kv_part.astype(jnp.bfloat16), CTX, -distance)
        kv_total = kv_total + returned.astype(jnp.float32)
    query_grad = normalize_back(
        query_in,
        query_inv,
        q_gain[0],
        unrotate(query_rot_grad.reshape(tok_rows, q_heads, HEAD), cosine, sine_table),
    )
    query_grad = query_grad.reshape(tok_rows, q_heads * HEAD).astype(jnp.bfloat16)
    key_back = normalize_back(key_in, key_inv, k_gain[0], unrotate(kv_total[0], cosine, sine_table))
    key_back = key_back.reshape(tok_rows, kv_width).astype(jnp.bfloat16)
    value_back = kv_total[1].reshape(tok_rows, kv_width).astype(jnp.bfloat16)
    both_back = jnp.concatenate([key_back, value_back], 1)
    group_back = gathered(both_back, "cb", row_parts)
    grad_rows = lax.psum_scatter(
        lax.dot_general(
            inputs_slice, group_back, (((0,), (0,)), ((), ())), preferred_element_type=jnp.float32
        ),
        "cz",
        scatter_dimension=0,
        tiled=True,
    )
    slice_grad = lax.dot_general(
        group_back, weight_slice, (((1,), (1,)), ((), ())), preferred_element_type=jnp.float32
    ).astype(jnp.bfloat16)
    input_grad = lax.all_to_all(slice_grad, "cb", 0, 1, tiled=True)
    passed = shifted(input_grad, "pipe", -1)
    return (
        query_grad[None],
        grad_rows[:, :kv_width][None],
        grad_rows[:, kv_width:][None],
        passed[None],
    )


CTX = ("cb", "cz")


def solution(mesh):
    col_parts = 8
    row_parts = mesh.shape["ctx"] // col_parts
    grid = mesh.devices.reshape(row_parts, col_parts, mesh.shape["pipe"])
    split_mesh = Mesh(grid, ("cb", "cz", "pipe"))
    rows = P("pipe", CTX, None)
    inner = jax.shard_map(
        functools.partial(local, row_parts=row_parts, col_parts=col_parts),
        mesh=split_mesh,
        in_specs=(rows, rows, rows, P("pipe", None), rows, rows, P("pipe", None), P("pipe", None)),
        out_specs=(rows, rows, rows, rows),
        check_vma=False,
    )
    placed = NamedSharding(mesh, P("pipe", "ctx", None))

    def run(*args):
        return tuple(lax.with_sharding_constraint(out, placed) for out in inner(*args))

    return run
```

```python
import jax
import jax.numpy as jnp
from jax import lax
import functools

from jax.sharding import Mesh, NamedSharding, PartitionSpec as P

HEAD = 128
WINDOW = 768


epsilon = 1e-06
theta_base = 1000000.0


def axis_count(axis):
    names = axis if isinstance(axis, tuple) else (axis,)
    count = 1
    for name in names:
        count *= lax.axis_size(name)
    return count


def passed_along(block, axis, distance):
    devices = range(axis_count(axis))
    route = [(i - distance, i) for i in devices if i - distance in devices]
    return lax.ppermute(block, axis, route)


def shifted(shard, axis, by):
    devices = axis_count(axis)
    return lax.ppermute(shard, axis, [(i, (i + by) % devices) for i in range(devices)])


def rope_tables(positions):
    half_width = HEAD // 2
    frequency = jnp.exp(
        jnp.arange(half_width, dtype=jnp.float32) * (-2.0 * jnp.log(jnp.float32(theta_base)) / HEAD)
    )
    angles = positions.astype(jnp.float32)[:, None] * frequency[None, :]
    return (jnp.cos(angles), jnp.sin(angles))


def rotate(values, cosine, sine_table):
    half_width = values.shape[-1] // 2
    front_half = values[..., :half_width]
    back_half = values[..., half_width:]
    cos_b = cosine[:, None, :]
    sin_b = sine_table[:, None, :]
    return jnp.concatenate(
        [front_half * cos_b - back_half * sin_b, back_half * cos_b + front_half * sin_b], -1
    )


def unrotate(upstream, cosine, sine_table):
    half_width = upstream.shape[-1] // 2
    front_half = upstream[..., :half_width]
    back_half = upstream[..., half_width:]
    cos_b = cosine[:, None, :]
    sin_b = sine_table[:, None, :]
    return jnp.concatenate(
        [front_half * cos_b + back_half * sin_b, back_half * cos_b - front_half * sin_b], -1
    )


def normalize(values, gain_row):
    inverse = lax.rsqrt(jnp.mean(values * values, -1, keepdims=True) + epsilon)
    return (values * inverse * gain_row, inverse)


def normalize_back(values, inverse, gain_row, upstream):
    scaled = upstream * gain_row
    cubed = inverse * inverse * inverse
    return inverse * scaled - values * cubed * jnp.mean(values * scaled, -1, keepdims=True)


def gathered(block, axis, parts):
    copies = jnp.broadcast_to(block[None], (parts,) + block.shape)
    received = lax.all_to_all(copies, axis, 0, 0, tiled=True)
    return received.reshape((parts * block.shape[0],) + block.shape[1:])


def summed_over(partial, axis, parts, sent_as):
    pieces = partial.astype(sent_as).reshape((parts, partial.shape[0] // parts) + partial.shape[1:])
    received = lax.all_to_all(pieces, axis, 0, 0, tiled=True)
    return jnp.sum(received.astype(jnp.float32), 0)


def relayed_blocks(own_pair, reach_blocks):
    blocks = [own_pair]
    step = 1
    while len(blocks) <= reach_blocks:
        sent = jnp.stack(blocks[: min(step, reach_blocks + 1 - step)])
        arrived = passed_along(sent, CTX, step)
        blocks = blocks + [arrived[k] for k in range(arrived.shape[0])]
        step *= 2
    return blocks[: reach_blocks + 1]


def relayed_sums(kv_parts, tok_rows, reach_blocks):
    sums = [kv_parts[:, :tok_rows]] + [
        kv_parts[:, d * tok_rows : (d + 1) * tok_rows].astype(jnp.bfloat16).astype(jnp.float32)
        for d in range(1, reach_blocks + 1)
    ]
    first = True
    step = 1
    while step * 2 <= reach_blocks:
        step *= 2
    while step >= 1:
        count = len(sums) - step
        sent = jnp.stack(sums[step:])
        if first:
            sent = sent.astype(jnp.bfloat16)
        arrived = passed_along(sent, CTX, -step).astype(jnp.float32)
        sums = [sums[k] + arrived[k] if k < count else sums[k] for k in range(step)]
        first = False
        step //= 2
    return sums[0]


def guarded(tile_work, operands):
    return tile_work(*operands)


def local(inputs, q_raw, grad_out, segments, w_key, w_value, q_gain, k_gain, row_parts, col_parts):
    tokens_here = inputs[0]
    tok_rows = tokens_here.shape[0]
    kv_width = w_key.shape[2]
    kv_heads = kv_width // HEAD
    q_heads = q_raw.shape[2] // HEAD
    group = q_heads // kv_heads
    score_scale = HEAD ** (-0.5)
    reach_blocks = WINDOW // tok_rows
    col_index = lax.axis_index("cz")
    ctx_index = lax.axis_index("cb") * col_parts + col_index
    both_rows = jnp.concatenate([w_key[0], w_value[0]], 1)
    weight_slice = lax.all_gather(both_rows, "cz", axis=0, tiled=True)
    inputs_slice = lax.all_to_all(tokens_here, "cb", 1, 0, tiled=True)
    projected = summed_over(
        jnp.dot(inputs_slice, weight_slice, preferred_element_type=jnp.float32),
        "cb",
        row_parts,
        jnp.bfloat16,
    )
    key_raw = projected[:, :kv_width].astype(jnp.bfloat16)
    value_own = projected[:, kv_width:].astype(jnp.bfloat16).reshape(tok_rows, kv_heads, HEAD)
    local_pos = jnp.arange(tok_rows, dtype=jnp.int32)
    positions = ctx_index * tok_rows + local_pos
    cosine, sine_table = rope_tables(positions)
    query_in = q_raw[0].astype(jnp.float32).reshape(tok_rows, q_heads, HEAD)
    query_norm, query_inv = normalize(query_in, q_gain[0])
    query_rot = rotate(query_norm, cosine, sine_table).astype(jnp.bfloat16)
    key_in = key_raw.astype(jnp.float32).reshape(tok_rows, kv_heads, HEAD)
    key_norm, key_inv = normalize(key_in, k_gain[0])
    key_rot = rotate(key_norm, cosine, sine_table).astype(jnp.bfloat16)
    own_pair = jnp.stack([key_rot, value_own])
    key_blocks = relayed_blocks(own_pair, reach_blocks)
    seg_all = segments[0]
    seg_query = lax.dynamic_slice_in_dim(seg_all, ctx_index * tok_rows, tok_rows)
    allowed_list = []
    for distance in range(reach_blocks + 1):
        key_pos = (ctx_index - distance) * tok_rows + local_pos
        seg_key = lax.dynamic_slice_in_dim(
            seg_all, jnp.maximum(ctx_index - distance, 0) * tok_rows, tok_rows
        )
        offset = positions[:, None] - key_pos[None, :]
        allowed = (
            (offset >= 0)
            & (offset < WINDOW)
            & (key_pos >= 0)[None, :]
            & (seg_query[:, None] == seg_key[None, :])
        )
        allowed_list.append(allowed)
    q_group = query_rot.reshape(tok_rows, kv_heads, group, HEAD)
    out_grad = grad_out[0].reshape(tok_rows, kv_heads, group, HEAD)
    pairs = jnp.concatenate(key_blocks, 1)
    keys, values = pairs[0], pairs[1]
    allowed = jnp.concatenate(allowed_list, 1)
    scores = (
        jnp.einsum("qgrd,kgd->grqk", q_group, keys, preferred_element_type=jnp.float32)
        * score_scale
    )
    exp_score = jnp.where(allowed, jnp.exp(scores), 0.0)
    row_total = jnp.sum(exp_score, -1, keepdims=True)
    prob_tile = (exp_score / row_total).astype(jnp.bfloat16)
    attn_out = jnp.einsum(
        "grqk,kgd->qgrd", prob_tile, values, preferred_element_type=jnp.float32
    )
    row_delta = jnp.sum(out_grad.astype(jnp.float32) * attn_out, -1).transpose(1, 2, 0)[..., None]
    prob_grad = jnp.einsum(
        "qgrd,kgd->grqk", out_grad, values, preferred_element_type=jnp.float32
    )
    score_grad = (prob_tile.astype(jnp.float32) * (prob_grad - row_delta)).astype(jnp.bfloat16)
    value_grad = jnp.einsum(
        "grqk,qgrd->kgd", prob_tile, out_grad, preferred_element_type=jnp.float32
    )
    key_grad = (
        jnp.einsum("grqk,qgrd->kgd", score_grad, q_group, preferred_element_type=jnp.float32)
        * score_scale
    )
    query_rot_grad = (
        jnp.einsum("grqk,kgd->qgrd", score_grad, keys, preferred_element_type=jnp.float32)
        * score_scale
    )
    kv_parts = jnp.stack([key_grad, value_grad])
    kv_total = relayed_sums(kv_parts, tok_rows, reach_blocks)
    query_grad = normalize_back(
        query_in,
        query_inv,
        q_gain[0],
        unrotate(query_rot_grad.reshape(tok_rows, q_heads, HEAD), cosine, sine_table),
    )
    query_grad = query_grad.reshape(tok_rows, q_heads * HEAD).astype(jnp.bfloat16)
    key_back = normalize_back(key_in, key_inv, k_gain[0], unrotate(kv_total[0], cosine, sine_table))
    key_back = key_back.reshape(tok_rows, kv_width).astype(jnp.bfloat16)
    value_back = kv_total[1].reshape(tok_rows, kv_width).astype(jnp.bfloat16)
    both_back = jnp.concatenate([key_back, value_back], 1)
    group_back = gathered(both_back, "cb", row_parts)
    grad_rows = lax.psum_scatter(
        lax.dot_general(
            inputs_slice, group_back, (((0,), (0,)), ((), ())), preferred_element_type=jnp.float32
        ),
        "cz",
        scatter_dimension=0,
        tiled=True,
    )
    slice_grad = lax.dot_general(
        group_back, weight_slice, (((1,), (1,)), ((), ())), preferred_element_type=jnp.float32
    ).astype(jnp.bfloat16)
    input_grad = lax.all_to_all(slice_grad, "cb", 0, 1, tiled=True)
    passed = shifted(input_grad, "pipe", -1)
    return (
        query_grad[None],
        grad_rows[:, :kv_width][None],
        grad_rows[:, kv_width:][None],
        passed[None],
    )


CTX = ("cb", "cz")


def solution(mesh):
    col_parts = 8
    row_parts = mesh.shape["ctx"] // col_parts
    grid = mesh.devices.reshape(row_parts, col_parts, mesh.shape["pipe"])
    split_mesh = Mesh(grid, ("cb", "cz", "pipe"))
    rows = P("pipe", CTX, None)
    inner = jax.shard_map(
        functools.partial(local, row_parts=row_parts, col_parts=col_parts),
        mesh=split_mesh,
        in_specs=(rows, rows, rows, P("pipe", None), rows, rows, P("pipe", None), P("pipe", None)),
        out_specs=(rows, rows, rows, rows),
        check_vma=False,
    )
    placed = NamedSharding(mesh, P("pipe", "ctx", None))

    def run(*args):
        return tuple(lax.with_sharding_constraint(out, placed) for out in inner(*args))

    return run
```

```python
import jax
import jax.numpy as jnp
from jax import lax
import functools

from jax.sharding import Mesh, NamedSharding, PartitionSpec as P

HEAD = 128
WINDOW = 768


epsilon = 1e-06
theta_base = 1000000.0


def axis_count(axis):
    names = axis if isinstance(axis, tuple) else (axis,)
    count = 1
    for name in names:
        count *= lax.axis_size(name)
    return count


def passed_along(block, axis, distance):
    devices = range(axis_count(axis))
    route = [(i - distance, i) for i in devices if i - distance in devices]
    return lax.ppermute(block, axis, route)


def shifted(shard, axis, by):
    devices = axis_count(axis)
    return lax.ppermute(shard, axis, [(i, (i + by) % devices) for i in range(devices)])


def rope_tables(positions):
    half_width = HEAD // 2
    frequency = jnp.exp(
        jnp.arange(half_width, dtype=jnp.float32) * (-2.0 * jnp.log(jnp.float32(theta_base)) / HEAD)
    )
    angles = positions.astype(jnp.float32)[:, None] * frequency[None, :]
    return (jnp.cos(angles), jnp.sin(angles))


def rotate(values, cosine, sine_table):
    half_width = values.shape[-1] // 2
    front_half = values[..., :half_width]
    back_half = values[..., half_width:]
    cos_b = cosine[:, None, :]
    sin_b = sine_table[:, None, :]
    return jnp.concatenate(
        [front_half * cos_b - back_half * sin_b, back_half * cos_b + front_half * sin_b], -1
    )


def unrotate(upstream, cosine, sine_table):
    half_width = upstream.shape[-1] // 2
    front_half = upstream[..., :half_width]
    back_half = upstream[..., half_width:]
    cos_b = cosine[:, None, :]
    sin_b = sine_table[:, None, :]
    return jnp.concatenate(
        [front_half * cos_b + back_half * sin_b, back_half * cos_b - front_half * sin_b], -1
    )


def normalize(values, gain_row):
    inverse = lax.rsqrt(jnp.mean(values * values, -1, keepdims=True) + epsilon)
    return (values * inverse * gain_row, inverse)


def normalize_back(values, inverse, gain_row, upstream):
    scaled = upstream * gain_row
    cubed = inverse * inverse * inverse
    return inverse * scaled - values * cubed * jnp.mean(values * scaled, -1, keepdims=True)


def gathered(block, axis, parts):
    copies = jnp.broadcast_to(block[None], (parts,) + block.shape)
    received = lax.all_to_all(copies, axis, 0, 0, tiled=True)
    return received.reshape((parts * block.shape[0],) + block.shape[1:])


def summed_over(partial, axis, parts, sent_as):
    pieces = partial.astype(sent_as).reshape((parts, partial.shape[0] // parts) + partial.shape[1:])
    received = lax.all_to_all(pieces, axis, 0, 0, tiled=True)
    return jnp.sum(received.astype(jnp.float32), 0)


def guarded(tile_work, operands):
    return tile_work(*operands)


def local(inputs, q_raw, grad_out, segments, w_key, w_value, q_gain, k_gain, row_parts, col_parts):
    tokens_here = inputs[0]
    tok_rows = tokens_here.shape[0]
    kv_width = w_key.shape[2]
    kv_heads = kv_width // HEAD
    q_heads = q_raw.shape[2] // HEAD
    group = q_heads // kv_heads
    score_scale = HEAD ** (-0.5)
    reach_blocks = WINDOW // tok_rows
    col_index = lax.axis_index("cz")
    ctx_index = lax.axis_index("cb") * col_parts + col_index
    both_rows = jnp.concatenate([w_key[0], w_value[0]], 1)
    weight_slice = lax.all_gather(both_rows, "cz", axis=0, tiled=True)
    inputs_slice = lax.all_to_all(tokens_here, "cb", 1, 0, tiled=True)
    projected = summed_over(
        jnp.dot(inputs_slice, weight_slice, preferred_element_type=jnp.float32),
        "cb",
        row_parts,
        jnp.bfloat16,
    )
    key_raw = projected[:, :kv_width].astype(jnp.bfloat16)
    value_own = projected[:, kv_width:].astype(jnp.bfloat16).reshape(tok_rows, kv_heads, HEAD)
    local_pos = jnp.arange(tok_rows, dtype=jnp.int32)
    positions = ctx_index * tok_rows + local_pos
    cosine, sine_table = rope_tables(positions)
    query_in = q_raw[0].astype(jnp.float32).reshape(tok_rows, q_heads, HEAD)
    query_norm, query_inv = normalize(query_in, q_gain[0])
    query_rot = rotate(query_norm, cosine, sine_table).astype(jnp.bfloat16)
    key_in = key_raw.astype(jnp.float32).reshape(tok_rows, kv_heads, HEAD)
    key_norm, key_inv = normalize(key_in, k_gain[0])
    key_rot = rotate(key_norm, cosine, sine_table).astype(jnp.bfloat16)
    own_pair = jnp.stack([key_rot, value_own])
    key_blocks = [own_pair]
    for distance in range(1, reach_blocks + 1):
        key_blocks.append(passed_along(own_pair, CTX, distance))
    seg_all = segments[0]
    seg_query = lax.dynamic_slice_in_dim(seg_all, ctx_index * tok_rows, tok_rows)
    allowed_list = []
    for distance in range(reach_blocks + 1):
        key_pos = (ctx_index - distance) * tok_rows + local_pos
        seg_key = lax.dynamic_slice_in_dim(
            seg_all, jnp.maximum(ctx_index - distance, 0) * tok_rows, tok_rows
        )
        offset = positions[:, None] - key_pos[None, :]
        allowed = (
            (offset >= 0)
            & (offset < WINDOW)
            & (key_pos >= 0)[None, :]
            & (seg_query[:, None] == seg_key[None, :])
        )
        allowed_list.append(allowed)
    q_group = query_rot.reshape(tok_rows, kv_heads, group, HEAD)
    out_grad = grad_out[0].reshape(tok_rows, kv_heads, group, HEAD)

    def exp_block(key_pair, allowed):
        scores = (
            jnp.einsum("qgrd,kgd->grqk", q_group, key_pair[0], preferred_element_type=jnp.float32)
            * score_scale
        )
        return jnp.where(allowed, jnp.exp(scores), 0.0)

    def total_block(key_pair, allowed):
        return jnp.sum(exp_block(key_pair, allowed), -1)

    zero_total = jnp.zeros((kv_heads, group, tok_rows), jnp.float32)
    row_total = zero_total
    for distance in range(reach_blocks + 1):
        row_total = row_total + guarded(total_block, (key_blocks[distance], allowed_list[distance]))

    def prob_block(key_pair, allowed):
        prob_tile = (exp_block(key_pair, allowed) / row_total[..., None]).astype(jnp.bfloat16)
        out_tile = jnp.einsum(
            "grqk,kgd->qgrd", prob_tile, key_pair[1], preferred_element_type=jnp.float32
        )
        return (prob_tile, out_tile)

    zero_query = jnp.zeros((tok_rows, kv_heads, group, HEAD), jnp.float32)
    prob_list = []
    attn_out = zero_query
    for distance in range(reach_blocks + 1):
        prob_tile, out_tile = guarded(prob_block, (key_blocks[distance], allowed_list[distance]))
        prob_list.append(prob_tile)
        attn_out = attn_out + out_tile
    row_delta = jnp.sum(out_grad.astype(jnp.float32) * attn_out, -1).transpose(1, 2, 0)[..., None]

    def grad_block(key_pair, prob_tile):
        prob_grad = jnp.einsum(
            "qgrd,kgd->grqk", out_grad, key_pair[1], preferred_element_type=jnp.float32
        )
        score_grad = (prob_tile.astype(jnp.float32) * (prob_grad - row_delta)).astype(jnp.bfloat16)
        value_grad = jnp.einsum(
            "grqk,qgrd->kgd", prob_tile, out_grad, preferred_element_type=jnp.float32
        )
        key_grad = (
            jnp.einsum("grqk,qgrd->kgd", score_grad, q_group, preferred_element_type=jnp.float32)
            * score_scale
        )
        return (score_grad, jnp.stack([key_grad, value_grad]))

    zero_pair = jnp.zeros((2, tok_rows, kv_heads, HEAD), jnp.float32)
    kv_total = zero_pair
    score_list = []
    for distance in range(reach_blocks + 1):
        score_grad, kv_part = guarded(grad_block, (key_blocks[distance], prob_list[distance]))
        score_list.append(score_grad)
        if distance == 0:
            kv_total = kv_part
        else:
            returned = passed_along(kv_part.astype(jnp.bfloat16), CTX, -distance)
            kv_total = kv_total + returned.astype(jnp.float32)
    key_back = normalize_back(key_in, key_inv, k_gain[0], unrotate(kv_total[0], cosine, sine_table))
    key_back = key_back.reshape(tok_rows, kv_width).astype(jnp.bfloat16)
    value_back = kv_total[1].reshape(tok_rows, kv_width).astype(jnp.bfloat16)
    both_back = jnp.concatenate([key_back, value_back], 1)
    group_back = gathered(both_back, "cb", row_parts)
    grad_rows = lax.psum_scatter(
        lax.dot_general(
            inputs_slice, group_back, (((0,), (0,)), ((), ())), preferred_element_type=jnp.float32
        ),
        "cz",
        scatter_dimension=0,
        tiled=True,
    )
    slice_grad = lax.dot_general(
        group_back, weight_slice, (((1,), (1,)), ((), ())), preferred_element_type=jnp.float32
    ).astype(jnp.bfloat16)
    score_list, slice_grad = lax.optimization_barrier((score_list, slice_grad))
    input_grad = lax.all_to_all(slice_grad, "cb", 0, 1, tiled=True)
    query_rot_grad = zero_query
    for distance in range(reach_blocks + 1):
        query_part = (
            jnp.einsum(
                "grqk,kgd->qgrd",
                score_list[distance],
                key_blocks[distance][0],
                preferred_element_type=jnp.float32,
            )
            * score_scale
        )
        query_rot_grad = query_rot_grad + query_part
    query_grad = normalize_back(
        query_in,
        query_inv,
        q_gain[0],
        unrotate(query_rot_grad.reshape(tok_rows, q_heads, HEAD), cosine, sine_table),
    )
    query_grad = query_grad.reshape(tok_rows, q_heads * HEAD).astype(jnp.bfloat16)
    passed = shifted(input_grad, "pipe", -1)
    return (
        query_grad[None],
        grad_rows[:, :kv_width][None],
        grad_rows[:, kv_width:][None],
        passed[None],
    )


CTX = ("cb", "cz")


def solution(mesh):
    col_parts = 8
    row_parts = mesh.shape["ctx"] // col_parts
    grid = mesh.devices.reshape(row_parts, col_parts, mesh.shape["pipe"])
    split_mesh = Mesh(grid, ("cb", "cz", "pipe"))
    rows = P("pipe", CTX, None)
    inner = jax.shard_map(
        functools.partial(local, row_parts=row_parts, col_parts=col_parts),
        mesh=split_mesh,
        in_specs=(rows, rows, rows, P("pipe", None), rows, rows, P("pipe", None), P("pipe", None)),
        out_specs=(rows, rows, rows, rows),
        check_vma=False,
    )
    placed = NamedSharding(mesh, P("pipe", "ctx", None))

    def run(*args):
        return tuple(lax.with_sharding_constraint(out, placed) for out in inner(*args))

    return run
```

```python
import jax
import jax.numpy as jnp
from jax import lax
import functools

from jax.sharding import Mesh, NamedSharding, PartitionSpec as P

HEAD = 128
WINDOW = 768


epsilon = 1e-06
theta_base = 1000000.0


def axis_count(axis):
    names = axis if isinstance(axis, tuple) else (axis,)
    count = 1
    for name in names:
        count *= lax.axis_size(name)
    return count


def passed_along(block, axis, distance):
    devices = range(axis_count(axis))
    route = [(i - distance, i) for i in devices if i - distance in devices]
    return lax.ppermute(block, axis, route)


def shifted(shard, axis, by):
    devices = axis_count(axis)
    return lax.ppermute(shard, axis, [(i, (i + by) % devices) for i in range(devices)])


def rope_tables(positions):
    half_width = HEAD // 2
    frequency = jnp.exp(
        jnp.arange(half_width, dtype=jnp.float32) * (-2.0 * jnp.log(jnp.float32(theta_base)) / HEAD)
    )
    angles = positions.astype(jnp.float32)[:, None] * frequency[None, :]
    return (jnp.cos(angles), jnp.sin(angles))


def rotate(values, cosine, sine_table):
    half_width = values.shape[-1] // 2
    front_half = values[..., :half_width]
    back_half = values[..., half_width:]
    cos_b = cosine[:, None, :]
    sin_b = sine_table[:, None, :]
    return jnp.concatenate(
        [front_half * cos_b - back_half * sin_b, back_half * cos_b + front_half * sin_b], -1
    )


def unrotate(upstream, cosine, sine_table):
    half_width = upstream.shape[-1] // 2
    front_half = upstream[..., :half_width]
    back_half = upstream[..., half_width:]
    cos_b = cosine[:, None, :]
    sin_b = sine_table[:, None, :]
    return jnp.concatenate(
        [front_half * cos_b + back_half * sin_b, back_half * cos_b - front_half * sin_b], -1
    )


def normalize(values, gain_row):
    inverse = lax.rsqrt(jnp.mean(values * values, -1, keepdims=True) + epsilon)
    return (values * inverse * gain_row, inverse)


def normalize_back(values, inverse, gain_row, upstream):
    scaled = upstream * gain_row
    cubed = inverse * inverse * inverse
    return inverse * scaled - values * cubed * jnp.mean(values * scaled, -1, keepdims=True)


def gathered(block, axis, parts):
    copies = jnp.broadcast_to(block[None], (parts,) + block.shape)
    received = lax.all_to_all(copies, axis, 0, 0, tiled=True)
    return received.reshape((parts * block.shape[0],) + block.shape[1:])


def summed_over(partial, axis, parts, sent_as):
    pieces = partial.astype(sent_as).reshape((parts, partial.shape[0] // parts) + partial.shape[1:])
    received = lax.all_to_all(pieces, axis, 0, 0, tiled=True)
    return jnp.sum(received.astype(jnp.float32), 0)


def guarded(tile_work, operands):
    return tile_work(*operands)


def local(inputs, q_raw, grad_out, segments, w_key, w_value, q_gain, k_gain, row_parts, col_parts):
    tokens_here = inputs[0]
    tok_rows = tokens_here.shape[0]
    kv_width = w_key.shape[2]
    kv_heads = kv_width // HEAD
    q_heads = q_raw.shape[2] // HEAD
    group = q_heads // kv_heads
    score_scale = HEAD ** (-0.5)
    reach_blocks = WINDOW // tok_rows
    col_index = lax.axis_index("cz")
    ctx_index = lax.axis_index("cb") * col_parts + col_index
    both_rows = jnp.concatenate([w_key[0], w_value[0]], 1)
    weight_slice = lax.all_gather(both_rows, "cz", axis=0, tiled=True)
    inputs_slice = lax.all_to_all(tokens_here, "cb", 1, 0, tiled=True)
    projected = summed_over(
        jnp.dot(inputs_slice, weight_slice, preferred_element_type=jnp.float32),
        "cb",
        row_parts,
        jnp.bfloat16,
    )
    key_raw = projected[:, :kv_width].astype(jnp.bfloat16)
    value_own = projected[:, kv_width:].astype(jnp.bfloat16).reshape(tok_rows, kv_heads, HEAD)
    local_pos = jnp.arange(tok_rows, dtype=jnp.int32)
    positions = ctx_index * tok_rows + local_pos
    cosine, sine_table = rope_tables(positions)
    query_in = q_raw[0].astype(jnp.float32).reshape(tok_rows, q_heads, HEAD)
    query_norm, query_inv = normalize(query_in, q_gain[0])
    query_rot = rotate(query_norm, cosine, sine_table).astype(jnp.bfloat16)
    key_in = key_raw.astype(jnp.float32).reshape(tok_rows, kv_heads, HEAD)
    key_norm, key_inv = normalize(key_in, k_gain[0])
    key_rot = rotate(key_norm, cosine, sine_table).astype(jnp.bfloat16)
    own_pair = jnp.stack([key_rot, value_own])
    key_blocks = [own_pair]
    for distance in range(1, reach_blocks + 1):
        key_blocks.append(passed_along(own_pair, CTX, distance))
    seg_all = segments[0]
    seg_query = lax.dynamic_slice_in_dim(seg_all, ctx_index * tok_rows, tok_rows)
    allowed_list = []
    for distance in range(reach_blocks + 1):
        key_pos = (ctx_index - distance) * tok_rows + local_pos
        seg_key = lax.dynamic_slice_in_dim(
            seg_all, jnp.maximum(ctx_index - distance, 0) * tok_rows, tok_rows
        )
        offset = positions[:, None] - key_pos[None, :]
        allowed = (
            (offset >= 0)
            & (offset < WINDOW)
            & (key_pos >= 0)[None, :]
            & (seg_query[:, None] == seg_key[None, :])
        )
        allowed_list.append(allowed)
    q_group = query_rot.reshape(tok_rows, kv_heads, group, HEAD)
    out_grad = grad_out[0].reshape(tok_rows, kv_heads, group, HEAD)

    def exp_block(key_pair, allowed):
        scores = (
            jnp.einsum("qgrd,kgd->grqk", q_group, key_pair[0], preferred_element_type=jnp.float32)
            * score_scale
        )
        return jnp.where(allowed, jnp.exp(scores), 0.0)

    def total_block(key_pair, allowed):
        return jnp.sum(exp_block(key_pair, allowed), -1)

    zero_total = jnp.zeros((kv_heads, group, tok_rows), jnp.float32)
    row_total = zero_total
    for distance in range(reach_blocks + 1):
        row_total = row_total + guarded(total_block, (key_blocks[distance], allowed_list[distance]))

    def prob_block(key_pair, allowed):
        prob_tile = (exp_block(key_pair, allowed) / row_total[..., None]).astype(jnp.bfloat16)
        out_tile = jnp.einsum(
            "grqk,kgd->qgrd", prob_tile, key_pair[1], preferred_element_type=jnp.float32
        )
        return (prob_tile, out_tile)

    zero_query = jnp.zeros((tok_rows, kv_heads, group, HEAD), jnp.float32)
    prob_list = []
    attn_out = zero_query
    for distance in range(reach_blocks + 1):
        prob_tile, out_tile = guarded(prob_block, (key_blocks[distance], allowed_list[distance]))
        prob_list.append(prob_tile)
        attn_out = attn_out + out_tile
    row_delta = jnp.sum(out_grad.astype(jnp.float32) * attn_out, -1).transpose(1, 2, 0)[..., None]

    def grad_block(key_pair, prob_tile):
        prob_grad = jnp.einsum(
            "qgrd,kgd->grqk", out_grad, key_pair[1], preferred_element_type=jnp.float32
        )
        score_grad = (prob_tile.astype(jnp.float32) * (prob_grad - row_delta)).astype(jnp.bfloat16)
        value_grad = jnp.einsum(
            "grqk,qgrd->kgd", prob_tile, out_grad, preferred_element_type=jnp.float32
        )
        key_grad = (
            jnp.einsum("grqk,qgrd->kgd", score_grad, q_group, preferred_element_type=jnp.float32)
            * score_scale
        )
        return (score_grad, jnp.stack([key_grad, value_grad]))

    zero_pair = jnp.zeros((2, tok_rows, kv_heads, HEAD), jnp.float32)
    kv_total = zero_pair
    score_list = []
    for distance in range(reach_blocks + 1):
        score_grad, kv_part = guarded(grad_block, (key_blocks[distance], prob_list[distance]))
        score_list.append(score_grad)
        if distance == 0:
            kv_total = kv_part
        else:
            returned = passed_along(kv_part.astype(jnp.bfloat16), CTX, -distance)
            kv_total = kv_total + returned.astype(jnp.float32)
    key_back = normalize_back(key_in, key_inv, k_gain[0], unrotate(kv_total[0], cosine, sine_table))
    key_back = key_back.reshape(tok_rows, kv_width).astype(jnp.bfloat16)
    value_back = kv_total[1].reshape(tok_rows, kv_width).astype(jnp.bfloat16)
    both_back = jnp.concatenate([key_back, value_back], 1)
    group_back = gathered(both_back, "cb", row_parts)
    grad_rows = lax.psum_scatter(
        lax.dot_general(
            inputs_slice, group_back, (((0,), (0,)), ((), ())), preferred_element_type=jnp.float32
        ).astype(jnp.bfloat16),
        "cz",
        scatter_dimension=0,
        tiled=True,
    ).astype(jnp.float32)
    slice_grad = lax.dot_general(
        group_back, weight_slice, (((1,), (1,)), ((), ())), preferred_element_type=jnp.float32
    ).astype(jnp.bfloat16)
    score_list, slice_grad = lax.optimization_barrier((score_list, slice_grad))
    input_grad = lax.all_to_all(
        slice_grad.reshape(row_parts, tok_rows, slice_grad.shape[1]), "cb", 0, 0, tiled=True
    )
    query_rot_grad = zero_query
    for distance in range(reach_blocks + 1):
        query_part = (
            jnp.einsum(
                "grqk,kgd->qgrd",
                score_list[distance],
                key_blocks[distance][0],
                preferred_element_type=jnp.float32,
            )
            * score_scale
        )
        query_rot_grad = query_rot_grad + query_part
    query_grad = normalize_back(
        query_in,
        query_inv,
        q_gain[0],
        unrotate(query_rot_grad.reshape(tok_rows, q_heads, HEAD), cosine, sine_table),
    )
    query_grad = query_grad.reshape(tok_rows, q_heads * HEAD).astype(jnp.bfloat16)
    passed = shifted(input_grad, "pipe", -1).transpose(1, 0, 2).reshape(tok_rows, -1)
    return (
        query_grad[None],
        grad_rows[:, :kv_width][None],
        grad_rows[:, kv_width:][None],
        passed[None],
    )


CTX = ("cb", "cz")


def solution(mesh):
    col_parts = 8
    row_parts = mesh.shape["ctx"] // col_parts
    grid = mesh.devices.reshape(row_parts, col_parts, mesh.shape["pipe"])
    split_mesh = Mesh(grid, ("cb", "cz", "pipe"))
    rows = P("pipe", CTX, None)
    inner = jax.shard_map(
        functools.partial(local, row_parts=row_parts, col_parts=col_parts),
        mesh=split_mesh,
        in_specs=(rows, rows, rows, P("pipe", None), rows, rows, P("pipe", None), P("pipe", None)),
        out_specs=(rows, rows, rows, rows),
        check_vma=False,
    )
    placed = NamedSharding(mesh, P("pipe", "ctx", None))

    def run(*args):
        return tuple(lax.with_sharding_constraint(out, placed) for out in inner(*args))

    return run
```

```python
import jax
import jax.numpy as jnp
from jax import lax
import functools

from jax.sharding import Mesh, NamedSharding, PartitionSpec as P

HEAD = 128
WINDOW = 768


epsilon = 1e-06
theta_base = 1000000.0


def axis_count(axis):
    names = axis if isinstance(axis, tuple) else (axis,)
    count = 1
    for name in names:
        count *= lax.axis_size(name)
    return count


def passed_along(block, axis, distance):
    devices = range(axis_count(axis))
    route = [(i - distance, i) for i in devices if i - distance in devices]
    return lax.ppermute(block, axis, route)


def shifted(shard, axis, by):
    devices = axis_count(axis)
    return lax.ppermute(shard, axis, [(i, (i + by) % devices) for i in range(devices)])


def rope_tables(positions):
    half_width = HEAD // 2
    frequency = jnp.exp(
        jnp.arange(half_width, dtype=jnp.float32) * (-2.0 * jnp.log(jnp.float32(theta_base)) / HEAD)
    )
    angles = positions.astype(jnp.float32)[:, None] * frequency[None, :]
    return (jnp.cos(angles), jnp.sin(angles))


def rotate(values, cosine, sine_table):
    half_width = values.shape[-1] // 2
    front_half = values[..., :half_width]
    back_half = values[..., half_width:]
    cos_b = cosine[:, None, :]
    sin_b = sine_table[:, None, :]
    return jnp.concatenate(
        [front_half * cos_b - back_half * sin_b, back_half * cos_b + front_half * sin_b], -1
    )


def unrotate(upstream, cosine, sine_table):
    half_width = upstream.shape[-1] // 2
    front_half = upstream[..., :half_width]
    back_half = upstream[..., half_width:]
    cos_b = cosine[:, None, :]
    sin_b = sine_table[:, None, :]
    return jnp.concatenate(
        [front_half * cos_b + back_half * sin_b, back_half * cos_b - front_half * sin_b], -1
    )


def normalize(values, gain_row):
    inverse = lax.rsqrt(jnp.mean(values * values, -1, keepdims=True) + epsilon)
    return (values * inverse * gain_row, inverse)


def normalize_back(values, inverse, gain_row, upstream):
    scaled = upstream * gain_row
    cubed = inverse * inverse * inverse
    return inverse * scaled - values * cubed * jnp.mean(values * scaled, -1, keepdims=True)


def gathered(block, axis, parts):
    copies = jnp.broadcast_to(block[None], (parts,) + block.shape)
    received = lax.all_to_all(copies, axis, 0, 0, tiled=True)
    return received.reshape((parts * block.shape[0],) + block.shape[1:])


def summed_over(partial, axis, parts, sent_as):
    pieces = partial.astype(sent_as).reshape((parts, partial.shape[0] // parts) + partial.shape[1:])
    received = lax.all_to_all(pieces, axis, 0, 0, tiled=True)
    return jnp.sum(received.astype(jnp.float32), 0)


def guarded(tile_work, operands):
    return tile_work(*operands)


def local(inputs, q_raw, grad_out, segments, w_key, w_value, q_gain, k_gain, row_parts, col_parts):
    tokens_here = inputs[0]
    tok_rows = tokens_here.shape[0]
    kv_width = w_key.shape[2]
    kv_heads = kv_width // HEAD
    q_heads = q_raw.shape[2] // HEAD
    group = q_heads // kv_heads
    score_scale = HEAD ** (-0.5)
    reach_blocks = WINDOW // tok_rows
    col_index = lax.axis_index("cz")
    ctx_index = lax.axis_index("cb") * col_parts + col_index
    both_rows = jnp.concatenate([w_key[0], w_value[0]], 1)
    weight_slice = lax.all_gather(both_rows, "cz", axis=0, tiled=True)
    inputs_slice = lax.all_to_all(tokens_here, "cb", 1, 0, tiled=True)
    projected = summed_over(
        jnp.dot(inputs_slice, weight_slice, preferred_element_type=jnp.float32),
        "cb",
        row_parts,
        jnp.bfloat16,
    )
    key_raw = projected[:, :kv_width].astype(jnp.bfloat16)
    value_own = projected[:, kv_width:].astype(jnp.bfloat16).reshape(tok_rows, kv_heads, HEAD)
    local_pos = jnp.arange(tok_rows, dtype=jnp.int32)
    positions = ctx_index * tok_rows + local_pos
    cosine, sine_table = rope_tables(positions)
    query_in = q_raw[0].astype(jnp.float32).reshape(tok_rows, q_heads, HEAD)
    query_norm, query_inv = normalize(query_in, q_gain[0])
    query_rot = rotate(query_norm, cosine, sine_table).astype(jnp.bfloat16)
    key_in = key_raw.astype(jnp.float32).reshape(tok_rows, kv_heads, HEAD)
    key_norm, key_inv = normalize(key_in, k_gain[0])
    key_rot = rotate(key_norm, cosine, sine_table).astype(jnp.bfloat16)
    own_pair = jnp.stack([key_rot, value_own])
    key_blocks = [own_pair]
    for distance in range(1, reach_blocks + 1):
        key_blocks.append(passed_along(own_pair, CTX, distance))
    seg_all = segments[0]
    seg_query = lax.dynamic_slice_in_dim(seg_all, ctx_index * tok_rows, tok_rows)
    allowed_list = []
    for distance in range(reach_blocks + 1):
        key_pos = (ctx_index - distance) * tok_rows + local_pos
        seg_key = lax.dynamic_slice_in_dim(
            seg_all, jnp.maximum(ctx_index - distance, 0) * tok_rows, tok_rows
        )
        offset = positions[:, None] - key_pos[None, :]
        allowed = (
            (offset >= 0)
            & (offset < WINDOW)
            & (key_pos >= 0)[None, :]
            & (seg_query[:, None] == seg_key[None, :])
        )
        allowed_list.append(allowed)
    q_group = query_rot.reshape(tok_rows, kv_heads, group, HEAD)
    out_grad = grad_out[0].reshape(tok_rows, kv_heads, group, HEAD)

    def exp_block(key_pair, allowed):
        scores = (
            jnp.einsum("qgrd,kgd->grqk", q_group, key_pair[0], preferred_element_type=jnp.float32)
            * score_scale
        )
        return jnp.where(allowed, jnp.exp(scores), 0.0)

    def total_block(key_pair, allowed):
        return jnp.sum(exp_block(key_pair, allowed), -1)

    zero_total = jnp.zeros((kv_heads, group, tok_rows), jnp.float32)
    row_total = zero_total
    for distance in range(reach_blocks + 1):
        row_total = row_total + guarded(total_block, (key_blocks[distance], allowed_list[distance]))

    def prob_block(key_pair, allowed):
        prob_tile = (exp_block(key_pair, allowed) / row_total[..., None]).astype(jnp.bfloat16)
        out_tile = jnp.einsum(
            "grqk,kgd->qgrd", prob_tile, key_pair[1], preferred_element_type=jnp.float32
        )
        return (prob_tile, out_tile)

    zero_query = jnp.zeros((tok_rows, kv_heads, group, HEAD), jnp.float32)
    prob_list = []
    attn_out = zero_query
    for distance in range(reach_blocks + 1):
        prob_tile, out_tile = guarded(prob_block, (key_blocks[distance], allowed_list[distance]))
        prob_list.append(prob_tile)
        attn_out = attn_out + out_tile
    row_delta = jnp.sum(out_grad.astype(jnp.float32) * attn_out, -1).transpose(1, 2, 0)[..., None]

    def grad_block(key_pair, prob_tile):
        prob_grad = jnp.einsum(
            "qgrd,kgd->grqk", out_grad, key_pair[1], preferred_element_type=jnp.float32
        )
        score_grad = (prob_tile.astype(jnp.float32) * (prob_grad - row_delta)).astype(jnp.bfloat16)
        value_grad = jnp.einsum(
            "grqk,qgrd->kgd", prob_tile, out_grad, preferred_element_type=jnp.float32
        )
        key_grad = (
            jnp.einsum("grqk,qgrd->kgd", score_grad, q_group, preferred_element_type=jnp.float32)
            * score_scale
        )
        return (score_grad, jnp.stack([key_grad, value_grad]))

    zero_pair = jnp.zeros((2, tok_rows, kv_heads, HEAD), jnp.float32)
    kv_total = zero_pair
    score_list = []
    for distance in range(reach_blocks + 1):
        score_grad, kv_part = guarded(grad_block, (key_blocks[distance], prob_list[distance]))
        score_list.append(score_grad)
        if distance == 0:
            kv_total = kv_part
        else:
            returned = passed_along(kv_part.astype(jnp.bfloat16), CTX, -distance)
            kv_total = kv_total + returned.astype(jnp.float32)
    key_back = normalize_back(key_in, key_inv, k_gain[0], unrotate(kv_total[0], cosine, sine_table))
    key_back = key_back.reshape(tok_rows, kv_width).astype(jnp.bfloat16)
    value_back = kv_total[1].reshape(tok_rows, kv_width).astype(jnp.bfloat16)
    both_back = jnp.concatenate([key_back, value_back], 1)
    group_back = gathered(both_back, "cb", row_parts)
    weight_part = lax.dot_general(
        inputs_slice, group_back, (((0,), (0,)), ((), ())), preferred_element_type=jnp.float32
    )
    weight_part, group_back = lax.optimization_barrier((weight_part, group_back))
    grad_rows = lax.psum_scatter(weight_part, "cz", scatter_dimension=0, tiled=True)
    slice_grad = lax.dot_general(
        group_back, weight_slice, (((1,), (1,)), ((), ())), preferred_element_type=jnp.float32
    ).astype(jnp.bfloat16)
    score_list, slice_grad = lax.optimization_barrier((score_list, slice_grad))
    input_grad = lax.all_to_all(
        slice_grad.reshape(row_parts, tok_rows, slice_grad.shape[1]), "cb", 0, 0, tiled=True
    )
    query_rot_grad = zero_query
    for distance in range(reach_blocks + 1):
        query_part = (
            jnp.einsum(
                "grqk,kgd->qgrd",
                score_list[distance],
                key_blocks[distance][0],
                preferred_element_type=jnp.float32,
            )
            * score_scale
        )
        query_rot_grad = query_rot_grad + query_part
    query_grad = normalize_back(
        query_in,
        query_inv,
        q_gain[0],
        unrotate(query_rot_grad.reshape(tok_rows, q_heads, HEAD), cosine, sine_table),
    )
    query_grad = query_grad.reshape(tok_rows, q_heads * HEAD).astype(jnp.bfloat16)
    passed = shifted(input_grad, "pipe", -1).transpose(1, 0, 2).reshape(tok_rows, -1)
    return (
        query_grad[None],
        grad_rows[:, :kv_width][None],
        grad_rows[:, kv_width:][None],
        passed[None],
    )


CTX = ("cb", "cz")


def solution(mesh):
    col_parts = 8
    row_parts = mesh.shape["ctx"] // col_parts
    grid = mesh.devices.reshape(row_parts, col_parts, mesh.shape["pipe"])
    split_mesh = Mesh(grid, ("cb", "cz", "pipe"))
    rows = P("pipe", CTX, None)
    inner = jax.shard_map(
        functools.partial(local, row_parts=row_parts, col_parts=col_parts),
        mesh=split_mesh,
        in_specs=(rows, rows, rows, P("pipe", None), rows, rows, P("pipe", None), P("pipe", None)),
        out_specs=(rows, rows, rows, rows),
        check_vma=False,
    )
    placed = NamedSharding(mesh, P("pipe", "ctx", None))

    def run(*args):
        return tuple(lax.with_sharding_constraint(out, placed) for out in inner(*args))

    return run
```

```python
import jax
import jax.numpy as jnp
from jax import lax
import functools

from jax.sharding import Mesh, NamedSharding, PartitionSpec as P

HEAD = 128
WINDOW = 768


epsilon = 1e-06
theta_base = 1000000.0


def axis_count(axis):
    names = axis if isinstance(axis, tuple) else (axis,)
    count = 1
    for name in names:
        count *= lax.axis_size(name)
    return count


def passed_along(block, axis, distance):
    devices = range(axis_count(axis))
    route = [(i - distance, i) for i in devices if i - distance in devices]
    return lax.ppermute(block, axis, route)


def shifted(shard, axis, by):
    devices = axis_count(axis)
    return lax.ppermute(shard, axis, [(i, (i + by) % devices) for i in range(devices)])


def rope_tables(positions):
    half_width = HEAD // 2
    frequency = jnp.exp(
        jnp.arange(half_width, dtype=jnp.float32) * (-2.0 * jnp.log(jnp.float32(theta_base)) / HEAD)
    )
    angles = positions.astype(jnp.float32)[:, None] * frequency[None, :]
    return (jnp.cos(angles), jnp.sin(angles))


def rotate(values, cosine, sine_table):
    half_width = values.shape[-1] // 2
    front_half = values[..., :half_width]
    back_half = values[..., half_width:]
    cos_b = cosine[:, None, :]
    sin_b = sine_table[:, None, :]
    return jnp.concatenate(
        [front_half * cos_b - back_half * sin_b, back_half * cos_b + front_half * sin_b], -1
    )


def unrotate(upstream, cosine, sine_table):
    half_width = upstream.shape[-1] // 2
    front_half = upstream[..., :half_width]
    back_half = upstream[..., half_width:]
    cos_b = cosine[:, None, :]
    sin_b = sine_table[:, None, :]
    return jnp.concatenate(
        [front_half * cos_b + back_half * sin_b, back_half * cos_b - front_half * sin_b], -1
    )


def normalize(values, gain_row):
    inverse = lax.rsqrt(jnp.mean(values * values, -1, keepdims=True) + epsilon)
    return (values * inverse * gain_row, inverse)


def normalize_back(values, inverse, gain_row, upstream):
    scaled = upstream * gain_row
    cubed = inverse * inverse * inverse
    return inverse * scaled - values * cubed * jnp.mean(values * scaled, -1, keepdims=True)


def gathered(block, axis, parts):
    copies = jnp.broadcast_to(block[None], (parts,) + block.shape)
    received = lax.all_to_all(copies, axis, 0, 0, tiled=True)
    return received.reshape((parts * block.shape[0],) + block.shape[1:])


def summed_over(partial, axis, parts, sent_as):
    pieces = partial.astype(sent_as).reshape((parts, partial.shape[0] // parts) + partial.shape[1:])
    received = lax.all_to_all(pieces, axis, 0, 0, tiled=True)
    return jnp.sum(received.astype(jnp.float32), 0)


def guarded(tile_work, operands):
    return tile_work(*operands)


def local(inputs, q_raw, grad_out, segments, w_key, w_value, q_gain, k_gain, row_parts, col_parts):
    tokens_here = inputs[0]
    tok_rows = tokens_here.shape[0]
    kv_width = w_key.shape[2]
    kv_heads = kv_width // HEAD
    q_heads = q_raw.shape[2] // HEAD
    group = q_heads // kv_heads
    score_scale = HEAD ** (-0.5)
    reach_blocks = WINDOW // tok_rows
    col_index = lax.axis_index("cz")
    ctx_index = lax.axis_index("cb") * col_parts + col_index
    both_rows = jnp.concatenate([w_key[0], w_value[0]], 1)
    weight_slice = lax.all_gather(both_rows, "cz", axis=0, tiled=True)
    inputs_slice = lax.all_to_all(tokens_here, "cb", 1, 0, tiled=True)
    projected = summed_over(
        jnp.dot(inputs_slice, weight_slice, preferred_element_type=jnp.float32),
        "cb",
        row_parts,
        jnp.bfloat16,
    )
    key_raw = projected[:, :kv_width].astype(jnp.bfloat16)
    value_own = projected[:, kv_width:].astype(jnp.bfloat16).reshape(tok_rows, kv_heads, HEAD)
    local_pos = jnp.arange(tok_rows, dtype=jnp.int32)
    positions = ctx_index * tok_rows + local_pos
    cosine, sine_table = rope_tables(positions)
    query_in = q_raw[0].astype(jnp.float32).reshape(tok_rows, q_heads, HEAD)
    query_norm, query_inv = normalize(query_in, q_gain[0])
    query_rot = rotate(query_norm, cosine, sine_table).astype(jnp.bfloat16)
    key_in = key_raw.astype(jnp.float32).reshape(tok_rows, kv_heads, HEAD)
    key_norm, key_inv = normalize(key_in, k_gain[0])
    key_rot = rotate(key_norm, cosine, sine_table).astype(jnp.bfloat16)
    own_pair = jnp.stack([key_rot, value_own])
    key_blocks = [own_pair]
    for distance in range(1, reach_blocks + 1):
        key_blocks.append(passed_along(own_pair, CTX, distance))
    seg_all = segments[0]
    seg_query = lax.dynamic_slice_in_dim(seg_all, ctx_index * tok_rows, tok_rows)
    allowed_list = []
    for distance in range(reach_blocks + 1):
        key_pos = (ctx_index - distance) * tok_rows + local_pos
        seg_key = lax.dynamic_slice_in_dim(
            seg_all, jnp.maximum(ctx_index - distance, 0) * tok_rows, tok_rows
        )
        offset = positions[:, None] - key_pos[None, :]
        allowed = (
            (offset >= 0)
            & (offset < WINDOW)
            & (key_pos >= 0)[None, :]
            & (seg_query[:, None] == seg_key[None, :])
        )
        allowed_list.append(allowed)
    q_group = query_rot.reshape(tok_rows, kv_heads, group, HEAD)
    out_grad = grad_out[0].reshape(tok_rows, kv_heads, group, HEAD)

    def exp_block(key_pair, allowed):
        scores = (
            jnp.einsum("qgrd,kgd->grqk", q_group, key_pair[0], preferred_element_type=jnp.float32)
            * score_scale
        )
        return jnp.where(allowed, jnp.exp(scores), 0.0)

    def total_block(key_pair, allowed):
        return jnp.sum(exp_block(key_pair, allowed), -1)

    zero_total = jnp.zeros((kv_heads, group, tok_rows), jnp.float32)
    row_total = zero_total
    for distance in range(reach_blocks + 1):
        row_total = row_total + guarded(total_block, (key_blocks[distance], allowed_list[distance]))

    def prob_block(key_pair, allowed):
        prob_tile = (exp_block(key_pair, allowed) / row_total[..., None]).astype(jnp.bfloat16)
        out_tile = jnp.einsum(
            "grqk,kgd->qgrd", prob_tile, key_pair[1], preferred_element_type=jnp.float32
        )
        return (prob_tile, out_tile)

    zero_query = jnp.zeros((tok_rows, kv_heads, group, HEAD), jnp.float32)
    prob_all, attn_out = prob_block(jnp.concatenate(key_blocks, 1), jnp.concatenate(allowed_list, 1))
    prob_list = [
        prob_all[..., d * tok_rows : (d + 1) * tok_rows] for d in range(reach_blocks + 1)
    ]
    row_delta = jnp.sum(out_grad.astype(jnp.float32) * attn_out, -1).transpose(1, 2, 0)[..., None]

    def grad_block(key_pair, prob_tile):
        prob_grad = jnp.einsum(
            "qgrd,kgd->grqk", out_grad, key_pair[1], preferred_element_type=jnp.float32
        )
        score_grad = (prob_tile.astype(jnp.float32) * (prob_grad - row_delta)).astype(jnp.bfloat16)
        value_grad = jnp.einsum(
            "grqk,qgrd->kgd", prob_tile, out_grad, preferred_element_type=jnp.float32
        )
        key_grad = (
            jnp.einsum("grqk,qgrd->kgd", score_grad, q_group, preferred_element_type=jnp.float32)
            * score_scale
        )
        return (score_grad, jnp.stack([key_grad, value_grad]))

    zero_pair = jnp.zeros((2, tok_rows, kv_heads, HEAD), jnp.float32)
    kv_total = zero_pair
    score_all, kv_all = grad_block(jnp.concatenate(key_blocks, 1), prob_all)
    score_list = [
        score_all[..., d * tok_rows : (d + 1) * tok_rows] for d in range(reach_blocks + 1)
    ]
    for distance in range(reach_blocks + 1):
        kv_part = kv_all[:, distance * tok_rows : (distance + 1) * tok_rows]
        if distance == 0:
            kv_total = kv_part
        else:
            returned = passed_along(kv_part.astype(jnp.bfloat16), CTX, -distance)
            kv_total = kv_total + returned.astype(jnp.float32)
    key_back = normalize_back(key_in, key_inv, k_gain[0], unrotate(kv_total[0], cosine, sine_table))
    key_back = key_back.reshape(tok_rows, kv_width).astype(jnp.bfloat16)
    value_back = kv_total[1].reshape(tok_rows, kv_width).astype(jnp.bfloat16)
    both_back = jnp.concatenate([key_back, value_back], 1)
    group_back = gathered(both_back, "cb", row_parts)
    weight_part = lax.dot_general(
        inputs_slice, group_back, (((0,), (0,)), ((), ())), preferred_element_type=jnp.float32
    )
    weight_part, group_back = lax.optimization_barrier((weight_part, group_back))
    grad_rows = lax.psum_scatter(weight_part, "cz", scatter_dimension=0, tiled=True)
    slice_grad = lax.dot_general(
        group_back, weight_slice, (((1,), (1,)), ((), ())), preferred_element_type=jnp.float32
    ).astype(jnp.bfloat16)
    score_list, slice_grad = lax.optimization_barrier((score_list, slice_grad))
    input_grad = lax.all_to_all(
        slice_grad.reshape(row_parts, tok_rows, slice_grad.shape[1]), "cb", 0, 0, tiled=True
    )
    query_rot_grad = (
        jnp.einsum(
            "grqk,kgd->qgrd",
            jnp.concatenate(score_list, -1),
            jnp.concatenate([pair[0] for pair in key_blocks], 0),
            preferred_element_type=jnp.float32,
        )
        * score_scale
    )
    query_grad = normalize_back(
        query_in,
        query_inv,
        q_gain[0],
        unrotate(query_rot_grad.reshape(tok_rows, q_heads, HEAD), cosine, sine_table),
    )
    query_grad = query_grad.reshape(tok_rows, q_heads * HEAD).astype(jnp.bfloat16)
    passed = shifted(input_grad, "pipe", -1).transpose(1, 0, 2).reshape(tok_rows, -1)
    return (
        query_grad[None],
        grad_rows[:, :kv_width][None],
        grad_rows[:, kv_width:][None],
        passed[None],
    )


CTX = ("cb", "cz")


def solution(mesh):
    col_parts = 8
    row_parts = mesh.shape["ctx"] // col_parts
    grid = mesh.devices.reshape(row_parts, col_parts, mesh.shape["pipe"])
    split_mesh = Mesh(grid, ("cb", "cz", "pipe"))
    rows = P("pipe", CTX, None)
    inner = jax.shard_map(
        functools.partial(local, row_parts=row_parts, col_parts=col_parts),
        mesh=split_mesh,
        in_specs=(rows, rows, rows, P("pipe", None), rows, rows, P("pipe", None), P("pipe", None)),
        out_specs=(rows, rows, rows, rows),
        check_vma=False,
    )
    placed = NamedSharding(mesh, P("pipe", "ctx", None))

    def run(*args):
        return tuple(lax.with_sharding_constraint(out, placed) for out in inner(*args))

    return run
```

```python
import jax
import jax.numpy as jnp
from jax import lax
import functools

from jax.sharding import Mesh, NamedSharding, PartitionSpec as P

HEAD = 128
WINDOW = 768


epsilon = 1e-06
theta_base = 1000000.0


def axis_count(axis):
    names = axis if isinstance(axis, tuple) else (axis,)
    count = 1
    for name in names:
        count *= lax.axis_size(name)
    return count


def passed_along(block, axis, distance):
    devices = range(axis_count(axis))
    route = [(i - distance, i) for i in devices if i - distance in devices]
    return lax.ppermute(block, axis, route)


def shifted(shard, axis, by):
    devices = axis_count(axis)
    return lax.ppermute(shard, axis, [(i, (i + by) % devices) for i in range(devices)])


def rope_tables(positions):
    half_width = HEAD // 2
    frequency = jnp.exp(
        jnp.arange(half_width, dtype=jnp.float32) * (-2.0 * jnp.log(jnp.float32(theta_base)) / HEAD)
    )
    angles = positions.astype(jnp.float32)[:, None] * frequency[None, :]
    return (jnp.cos(angles), jnp.sin(angles))


def rotate(values, cosine, sine_table):
    half_width = values.shape[-1] // 2
    front_half = values[..., :half_width]
    back_half = values[..., half_width:]
    cos_b = cosine[:, None, :]
    sin_b = sine_table[:, None, :]
    return jnp.concatenate(
        [front_half * cos_b - back_half * sin_b, back_half * cos_b + front_half * sin_b], -1
    )


def unrotate(upstream, cosine, sine_table):
    half_width = upstream.shape[-1] // 2
    front_half = upstream[..., :half_width]
    back_half = upstream[..., half_width:]
    cos_b = cosine[:, None, :]
    sin_b = sine_table[:, None, :]
    return jnp.concatenate(
        [front_half * cos_b + back_half * sin_b, back_half * cos_b - front_half * sin_b], -1
    )


def normalize(values, gain_row):
    inverse = lax.rsqrt(jnp.mean(values * values, -1, keepdims=True) + epsilon)
    return (values * inverse * gain_row, inverse)


def normalize_back(values, inverse, gain_row, upstream):
    scaled = upstream * gain_row
    cubed = inverse * inverse * inverse
    return inverse * scaled - values * cubed * jnp.mean(values * scaled, -1, keepdims=True)


def gathered(block, axis, parts):
    copies = jnp.broadcast_to(block[None], (parts,) + block.shape)
    received = lax.all_to_all(copies, axis, 0, 0, tiled=True)
    return received.reshape((parts * block.shape[0],) + block.shape[1:])


def summed_over(partial, axis, parts, sent_as):
    pieces = partial.astype(sent_as).reshape((parts, partial.shape[0] // parts) + partial.shape[1:])
    received = lax.all_to_all(pieces, axis, 0, 0, tiled=True)
    return jnp.sum(received.astype(jnp.float32), 0)


def guarded(tile_work, operands):
    return tile_work(*operands)


def local(inputs, q_raw, grad_out, segments, w_key, w_value, q_gain, k_gain, row_parts, col_parts):
    tokens_here = inputs[0]
    tok_rows = tokens_here.shape[0]
    kv_width = w_key.shape[2]
    kv_heads = kv_width // HEAD
    q_heads = q_raw.shape[2] // HEAD
    group = q_heads // kv_heads
    score_scale = HEAD ** (-0.5)
    reach_blocks = WINDOW // tok_rows
    col_index = lax.axis_index("cz")
    ctx_index = lax.axis_index("cb") * col_parts + col_index
    both_rows = jnp.concatenate([w_key[0], w_value[0]], 1)
    both_rows, tokens_here = lax.optimization_barrier((both_rows, tokens_here))
    weight_slice = lax.all_gather(both_rows, "cz", axis=0, tiled=True)
    inputs_slice = lax.all_to_all(tokens_here, "cb", 1, 0, tiled=True)
    projected = summed_over(
        jnp.dot(inputs_slice, weight_slice, preferred_element_type=jnp.float32),
        "cb",
        row_parts,
        jnp.bfloat16,
    )
    key_raw = projected[:, :kv_width].astype(jnp.bfloat16)
    value_own = projected[:, kv_width:].astype(jnp.bfloat16).reshape(tok_rows, kv_heads, HEAD)
    local_pos = jnp.arange(tok_rows, dtype=jnp.int32)
    positions = ctx_index * tok_rows + local_pos
    cosine, sine_table = rope_tables(positions)
    query_in = q_raw[0].astype(jnp.float32).reshape(tok_rows, q_heads, HEAD)
    query_norm, query_inv = normalize(query_in, q_gain[0])
    query_rot = rotate(query_norm, cosine, sine_table).astype(jnp.bfloat16)
    key_in = key_raw.astype(jnp.float32).reshape(tok_rows, kv_heads, HEAD)
    key_norm, key_inv = normalize(key_in, k_gain[0])
    key_rot = rotate(key_norm, cosine, sine_table).astype(jnp.bfloat16)
    own_pair = jnp.stack([key_rot, value_own])
    key_blocks = [own_pair]
    for distance in range(1, reach_blocks + 1):
        key_blocks.append(passed_along(own_pair, CTX, distance))
    seg_all = segments[0]
    seg_query = lax.dynamic_slice_in_dim(seg_all, ctx_index * tok_rows, tok_rows)
    allowed_list = []
    for distance in range(reach_blocks + 1):
        key_pos = (ctx_index - distance) * tok_rows + local_pos
        seg_key = lax.dynamic_slice_in_dim(
            seg_all, jnp.maximum(ctx_index - distance, 0) * tok_rows, tok_rows
        )
        offset = positions[:, None] - key_pos[None, :]
        allowed = (
            (offset >= 0)
            & (offset < WINDOW)
            & (key_pos >= 0)[None, :]
            & (seg_query[:, None] == seg_key[None, :])
        )
        allowed_list.append(allowed)
    q_group = query_rot.reshape(tok_rows, kv_heads, group, HEAD)
    out_grad = grad_out[0].reshape(tok_rows, kv_heads, group, HEAD)

    def exp_block(key_pair, allowed):
        scores = (
            jnp.einsum("qgrd,kgd->grqk", q_group, key_pair[0], preferred_element_type=jnp.float32)
            * score_scale
        )
        return jnp.where(allowed, jnp.exp(scores), 0.0)

    def total_block(key_pair, allowed):
        return jnp.sum(exp_block(key_pair, allowed), -1)

    zero_total = jnp.zeros((kv_heads, group, tok_rows), jnp.float32)
    row_total = zero_total
    for distance in range(reach_blocks + 1):
        row_total = row_total + guarded(total_block, (key_blocks[distance], allowed_list[distance]))

    def prob_block(key_pair, allowed):
        prob_tile = (exp_block(key_pair, allowed) / row_total[..., None]).astype(jnp.bfloat16)
        out_tile = jnp.einsum(
            "grqk,kgd->qgrd", prob_tile, key_pair[1], preferred_element_type=jnp.float32
        )
        return (prob_tile, out_tile)

    zero_query = jnp.zeros((tok_rows, kv_heads, group, HEAD), jnp.float32)
    prob_all, attn_out = prob_block(jnp.concatenate(key_blocks, 1), jnp.concatenate(allowed_list, 1))
    prob_list = [
        prob_all[..., d * tok_rows : (d + 1) * tok_rows] for d in range(reach_blocks + 1)
    ]
    row_delta = jnp.sum(out_grad.astype(jnp.float32) * attn_out, -1).transpose(1, 2, 0)[..., None]

    def grad_block(key_pair, prob_tile):
        prob_grad = jnp.einsum(
            "qgrd,kgd->grqk", out_grad, key_pair[1], preferred_element_type=jnp.float32
        )
        score_grad = (prob_tile.astype(jnp.float32) * (prob_grad - row_delta)).astype(jnp.bfloat16)
        value_grad = jnp.einsum(
            "grqk,qgrd->kgd", prob_tile, out_grad, preferred_element_type=jnp.float32
        )
        key_grad = (
            jnp.einsum("grqk,qgrd->kgd", score_grad, q_group, preferred_element_type=jnp.float32)
            * score_scale
        )
        return (score_grad, jnp.stack([key_grad, value_grad]))

    zero_pair = jnp.zeros((2, tok_rows, kv_heads, HEAD), jnp.float32)
    kv_total = zero_pair
    score_all, kv_all = grad_block(jnp.concatenate(key_blocks, 1), prob_all)
    score_list = [
        score_all[..., d * tok_rows : (d + 1) * tok_rows] for d in range(reach_blocks + 1)
    ]
    for distance in range(reach_blocks + 1):
        kv_part = kv_all[:, distance * tok_rows : (distance + 1) * tok_rows]
        if distance == 0:
            kv_total = kv_part
        else:
            returned = passed_along(kv_part.astype(jnp.bfloat16), CTX, -distance)
            kv_total = kv_total + returned.astype(jnp.float32)
    key_back = normalize_back(key_in, key_inv, k_gain[0], unrotate(kv_total[0], cosine, sine_table))
    key_back = key_back.reshape(tok_rows, kv_width).astype(jnp.bfloat16)
    value_back = kv_total[1].reshape(tok_rows, kv_width).astype(jnp.bfloat16)
    both_back = jnp.concatenate([key_back, value_back], 1)
    group_back = gathered(both_back, "cb", row_parts)
    weight_part = lax.dot_general(
        inputs_slice, group_back, (((0,), (0,)), ((), ())), preferred_element_type=jnp.float32
    )
    weight_part, group_back = lax.optimization_barrier((weight_part, group_back))
    grad_rows = lax.psum_scatter(weight_part, "cz", scatter_dimension=0, tiled=True)
    slice_grad = lax.dot_general(
        group_back, weight_slice, (((1,), (1,)), ((), ())), preferred_element_type=jnp.float32
    ).astype(jnp.bfloat16)
    score_list, slice_grad = lax.optimization_barrier((score_list, slice_grad))
    input_grad = lax.all_to_all(
        slice_grad.reshape(row_parts, tok_rows, slice_grad.shape[1]), "cb", 0, 0, tiled=True
    )
    query_rot_grad = (
        jnp.einsum(
            "grqk,kgd->qgrd",
            jnp.concatenate(score_list, -1),
            jnp.concatenate([pair[0] for pair in key_blocks], 0),
            preferred_element_type=jnp.float32,
        )
        * score_scale
    )
    query_grad = normalize_back(
        query_in,
        query_inv,
        q_gain[0],
        unrotate(query_rot_grad.reshape(tok_rows, q_heads, HEAD), cosine, sine_table),
    )
    query_grad = query_grad.reshape(tok_rows, q_heads * HEAD).astype(jnp.bfloat16)
    passed = shifted(input_grad, "pipe", -1).transpose(1, 0, 2).reshape(tok_rows, -1)
    return (
        query_grad[None],
        grad_rows[:, :kv_width][None],
        grad_rows[:, kv_width:][None],
        passed[None],
    )


CTX = ("cb", "cz")


def solution(mesh):
    col_parts = 8
    row_parts = mesh.shape["ctx"] // col_parts
    grid = mesh.devices.reshape(row_parts, col_parts, mesh.shape["pipe"])
    split_mesh = Mesh(grid, ("cb", "cz", "pipe"))
    rows = P("pipe", CTX, None)
    inner = jax.shard_map(
        functools.partial(local, row_parts=row_parts, col_parts=col_parts),
        mesh=split_mesh,
        in_specs=(rows, rows, rows, P("pipe", None), rows, rows, P("pipe", None), P("pipe", None)),
        out_specs=(rows, rows, rows, rows),
        check_vma=False,
    )
    placed = NamedSharding(mesh, P("pipe", "ctx", None))

    def run(*args):
        return tuple(lax.with_sharding_constraint(out, placed) for out in inner(*args))

    return run
```

```python
import jax
import jax.numpy as jnp
from jax import lax
import functools

from jax.experimental.layout import Layout, with_layout_constraint

from jax.sharding import Mesh, NamedSharding, PartitionSpec as P

HEAD = 128
WINDOW = 768


epsilon = 1e-06
theta_base = 1000000.0


def axis_count(axis):
    names = axis if isinstance(axis, tuple) else (axis,)
    count = 1
    for name in names:
        count *= lax.axis_size(name)
    return count


def passed_along(block, axis, distance):
    devices = range(axis_count(axis))
    route = [(i - distance, i) for i in devices if i - distance in devices]
    return lax.ppermute(block, axis, route)


def shifted(shard, axis, by):
    devices = axis_count(axis)
    return lax.ppermute(shard, axis, [(i, (i + by) % devices) for i in range(devices)])


def rope_tables(positions):
    half_width = HEAD // 2
    frequency = jnp.exp(
        jnp.arange(half_width, dtype=jnp.float32) * (-2.0 * jnp.log(jnp.float32(theta_base)) / HEAD)
    )
    angles = positions.astype(jnp.float32)[:, None] * frequency[None, :]
    return (jnp.cos(angles), jnp.sin(angles))


def rotate(values, cosine, sine_table):
    half_width = values.shape[-1] // 2
    front_half = values[..., :half_width]
    back_half = values[..., half_width:]
    cos_b = cosine[:, None, :]
    sin_b = sine_table[:, None, :]
    return jnp.concatenate(
        [front_half * cos_b - back_half * sin_b, back_half * cos_b + front_half * sin_b], -1
    )


def unrotate(upstream, cosine, sine_table):
    half_width = upstream.shape[-1] // 2
    front_half = upstream[..., :half_width]
    back_half = upstream[..., half_width:]
    cos_b = cosine[:, None, :]
    sin_b = sine_table[:, None, :]
    return jnp.concatenate(
        [front_half * cos_b + back_half * sin_b, back_half * cos_b - front_half * sin_b], -1
    )


def normalize(values, gain_row):
    inverse = lax.rsqrt(jnp.mean(values * values, -1, keepdims=True) + epsilon)
    return (values * inverse * gain_row, inverse)


def normalize_back(values, inverse, gain_row, upstream):
    scaled = upstream * gain_row
    cubed = inverse * inverse * inverse
    return inverse * scaled - values * cubed * jnp.mean(values * scaled, -1, keepdims=True)


def gathered(block, axis, parts):
    copies = jnp.broadcast_to(block[None], (parts,) + block.shape)
    received = lax.all_to_all(copies, axis, 0, 0, tiled=True)
    return received.reshape((parts * block.shape[0],) + block.shape[1:])


def summed_over(partial, axis, parts, sent_as):
    pieces = partial.astype(sent_as).reshape((parts, partial.shape[0] // parts) + partial.shape[1:])
    received = lax.all_to_all(pieces, axis, 0, 0, tiled=True)
    return jnp.sum(received.astype(jnp.float32), 0)


def guarded(tile_work, operands):
    return tile_work(*operands)


def local(inputs, q_raw, grad_out, segments, w_key, w_value, q_gain, k_gain, row_parts, col_parts):
    tokens_here = inputs[0]
    tok_rows = tokens_here.shape[0]
    kv_width = w_key.shape[2]
    kv_heads = kv_width // HEAD
    q_heads = q_raw.shape[2] // HEAD
    group = q_heads // kv_heads
    score_scale = HEAD ** (-0.5)
    reach_blocks = WINDOW // tok_rows
    col_index = lax.axis_index("cz")
    ctx_index = lax.axis_index("cb") * col_parts + col_index
    both_rows = jnp.concatenate([w_key[0], w_value[0]], 1)
    weight_slice = lax.all_gather(both_rows, "cz", axis=0, tiled=True)
    inputs_slice = lax.all_to_all(tokens_here, "cb", 1, 0, tiled=True)
    projected = summed_over(
        jnp.dot(inputs_slice, weight_slice, preferred_element_type=jnp.float32),
        "cb",
        row_parts,
        jnp.bfloat16,
    )
    key_raw = projected[:, :kv_width].astype(jnp.bfloat16)
    value_own = projected[:, kv_width:].astype(jnp.bfloat16).reshape(tok_rows, kv_heads, HEAD)
    local_pos = jnp.arange(tok_rows, dtype=jnp.int32)
    positions = ctx_index * tok_rows + local_pos
    cosine, sine_table = rope_tables(positions)
    query_in = q_raw[0].astype(jnp.float32).reshape(tok_rows, q_heads, HEAD)
    query_norm, query_inv = normalize(query_in, q_gain[0])
    query_rot = rotate(query_norm, cosine, sine_table).astype(jnp.bfloat16)
    key_in = key_raw.astype(jnp.float32).reshape(tok_rows, kv_heads, HEAD)
    key_norm, key_inv = normalize(key_in, k_gain[0])
    key_rot = rotate(key_norm, cosine, sine_table).astype(jnp.bfloat16)
    own_pair = jnp.stack([key_rot, value_own])
    key_blocks = [own_pair]
    for distance in range(1, reach_blocks + 1):
        key_blocks.append(passed_along(own_pair, CTX, distance))
    seg_all = segments[0]
    seg_query = lax.dynamic_slice_in_dim(seg_all, ctx_index * tok_rows, tok_rows)
    allowed_list = []
    for distance in range(reach_blocks + 1):
        key_pos = (ctx_index - distance) * tok_rows + local_pos
        seg_key = lax.dynamic_slice_in_dim(
            seg_all, jnp.maximum(ctx_index - distance, 0) * tok_rows, tok_rows
        )
        offset = positions[:, None] - key_pos[None, :]
        allowed = (
            (offset >= 0)
            & (offset < WINDOW)
            & (key_pos >= 0)[None, :]
            & (seg_query[:, None] == seg_key[None, :])
        )
        allowed_list.append(allowed)
    q_group = query_rot.reshape(tok_rows, kv_heads, group, HEAD)
    out_grad = grad_out[0].reshape(tok_rows, kv_heads, group, HEAD)

    def exp_block(key_pair, allowed):
        scores = (
            jnp.einsum("qgrd,kgd->grqk", q_group, key_pair[0], preferred_element_type=jnp.float32)
            * score_scale
        )
        return jnp.where(allowed, jnp.exp(scores), 0.0)

    def total_block(key_pair, allowed):
        return jnp.sum(exp_block(key_pair, allowed), -1)

    zero_total = jnp.zeros((kv_heads, group, tok_rows), jnp.float32)
    row_total = zero_total
    for distance in range(reach_blocks + 1):
        row_total = row_total + guarded(total_block, (key_blocks[distance], allowed_list[distance]))

    def prob_block(key_pair, allowed):
        prob_tile = (exp_block(key_pair, allowed) / row_total[..., None]).astype(jnp.bfloat16)
        out_tile = jnp.einsum(
            "grqk,kgd->qgrd", prob_tile, key_pair[1], preferred_element_type=jnp.float32
        )
        return (prob_tile, out_tile)

    zero_query = jnp.zeros((tok_rows, kv_heads, group, HEAD), jnp.float32)
    prob_list = []
    attn_out = zero_query
    for distance in range(reach_blocks + 1):
        prob_tile, out_tile = guarded(prob_block, (key_blocks[distance], allowed_list[distance]))
        prob_list.append(prob_tile)
        attn_out = attn_out + out_tile
    row_delta = jnp.sum(out_grad.astype(jnp.float32) * attn_out, -1).transpose(1, 2, 0)[..., None]

    def grad_block(key_pair, prob_tile):
        prob_grad = jnp.einsum(
            "qgrd,kgd->grqk", out_grad, key_pair[1], preferred_element_type=jnp.float32
        )
        score_grad = (prob_tile.astype(jnp.float32) * (prob_grad - row_delta)).astype(jnp.bfloat16)
        value_grad = jnp.einsum(
            "grqk,qgrd->kgd", prob_tile, out_grad, preferred_element_type=jnp.float32
        )
        key_grad = (
            jnp.einsum("grqk,qgrd->kgd", score_grad, q_group, preferred_element_type=jnp.float32)
            * score_scale
        )
        return (score_grad, jnp.stack([key_grad, value_grad]))

    zero_pair = jnp.zeros((2, tok_rows, kv_heads, HEAD), jnp.float32)
    kv_total = zero_pair
    score_list = []
    for distance in range(reach_blocks + 1):
        score_grad, kv_part = guarded(grad_block, (key_blocks[distance], prob_list[distance]))
        score_list.append(score_grad)
        if distance == 0:
            kv_total = kv_part
        else:
            returned = passed_along(kv_part.astype(jnp.bfloat16), CTX, -distance)
            kv_total = kv_total + returned.astype(jnp.float32)
    key_back = normalize_back(key_in, key_inv, k_gain[0], unrotate(kv_total[0], cosine, sine_table))
    key_back = key_back.reshape(tok_rows, kv_width).astype(jnp.bfloat16)
    value_back = kv_total[1].reshape(tok_rows, kv_width).astype(jnp.bfloat16)
    both_back = jnp.concatenate([key_back, value_back], 1)
    group_back = gathered(both_back, "cb", row_parts)
    group_back = with_layout_constraint(group_back, Layout(major_to_minor=(0, 1)))
    weight_part = lax.dot_general(
        inputs_slice, group_back, (((0,), (0,)), ((), ())), preferred_element_type=jnp.float32
    )
    weight_part, group_back = lax.optimization_barrier((weight_part, group_back))
    grad_rows = lax.psum_scatter(weight_part, "cz", scatter_dimension=0, tiled=True)
    slice_grad = lax.dot_general(
        group_back, weight_slice, (((1,), (1,)), ((), ())), preferred_element_type=jnp.float32
    ).astype(jnp.bfloat16)
    score_list, slice_grad = lax.optimization_barrier((score_list, slice_grad))
    input_grad = lax.all_to_all(
        slice_grad.reshape(row_parts, tok_rows, slice_grad.shape[1]), "cb", 0, 0, tiled=True
    )
    query_rot_grad = zero_query
    for distance in range(reach_blocks + 1):
        query_part = (
            jnp.einsum(
                "grqk,kgd->qgrd",
                score_list[distance],
                key_blocks[distance][0],
                preferred_element_type=jnp.float32,
            )
            * score_scale
        )
        query_rot_grad = query_rot_grad + query_part
    query_grad = normalize_back(
        query_in,
        query_inv,
        q_gain[0],
        unrotate(query_rot_grad.reshape(tok_rows, q_heads, HEAD), cosine, sine_table),
    )
    query_grad = query_grad.reshape(tok_rows, q_heads * HEAD).astype(jnp.bfloat16)
    passed = shifted(input_grad, "pipe", -1).transpose(1, 0, 2).reshape(tok_rows, -1)
    return (
        query_grad[None],
        grad_rows[:, :kv_width][None],
        grad_rows[:, kv_width:][None],
        passed[None],
    )


CTX = ("cb", "cz")


def solution(mesh):
    col_parts = 8
    row_parts = mesh.shape["ctx"] // col_parts
    grid = mesh.devices.reshape(row_parts, col_parts, mesh.shape["pipe"])
    split_mesh = Mesh(grid, ("cb", "cz", "pipe"))
    rows = P("pipe", CTX, None)
    inner = jax.shard_map(
        functools.partial(local, row_parts=row_parts, col_parts=col_parts),
        mesh=split_mesh,
        in_specs=(rows, rows, rows, P("pipe", None), rows, rows, P("pipe", None), P("pipe", None)),
        out_specs=(rows, rows, rows, rows),
        check_vma=False,
    )
    placed = NamedSharding(mesh, P("pipe", "ctx", None))

    def run(*args):
        return tuple(lax.with_sharding_constraint(out, placed) for out in inner(*args))

    return run
```

```python
import jax
import jax.numpy as jnp
from jax import lax
import functools

from jax.experimental.layout import Layout, with_layout_constraint

from jax.sharding import Mesh, NamedSharding, PartitionSpec as P

HEAD = 128
WINDOW = 768


epsilon = 1e-06
theta_base = 1000000.0


def axis_count(axis):
    names = axis if isinstance(axis, tuple) else (axis,)
    count = 1
    for name in names:
        count *= lax.axis_size(name)
    return count


def passed_along(block, axis, distance):
    devices = range(axis_count(axis))
    route = [(i - distance, i) for i in devices if i - distance in devices]
    return lax.ppermute(block, axis, route)


def shifted(shard, axis, by):
    devices = axis_count(axis)
    return lax.ppermute(shard, axis, [(i, (i + by) % devices) for i in range(devices)])


def rope_tables(positions):
    half_width = HEAD // 2
    frequency = jnp.exp(
        jnp.arange(half_width, dtype=jnp.float32) * (-2.0 * jnp.log(jnp.float32(theta_base)) / HEAD)
    )
    angles = positions.astype(jnp.float32)[:, None] * frequency[None, :]
    return (jnp.cos(angles), jnp.sin(angles))


def rotate(values, cosine, sine_table):
    half_width = values.shape[-1] // 2
    front_half = values[..., :half_width]
    back_half = values[..., half_width:]
    cos_b = cosine[:, None, :]
    sin_b = sine_table[:, None, :]
    return jnp.concatenate(
        [front_half * cos_b - back_half * sin_b, back_half * cos_b + front_half * sin_b], -1
    )


def unrotate(upstream, cosine, sine_table):
    half_width = upstream.shape[-1] // 2
    front_half = upstream[..., :half_width]
    back_half = upstream[..., half_width:]
    cos_b = cosine[:, None, :]
    sin_b = sine_table[:, None, :]
    return jnp.concatenate(
        [front_half * cos_b + back_half * sin_b, back_half * cos_b - front_half * sin_b], -1
    )


def normalize(values, gain_row):
    inverse = lax.rsqrt(jnp.mean(values * values, -1, keepdims=True) + epsilon)
    return (values * inverse * gain_row, inverse)


def normalize_back(values, inverse, gain_row, upstream):
    scaled = upstream * gain_row
    cubed = inverse * inverse * inverse
    return inverse * scaled - values * cubed * jnp.mean(values * scaled, -1, keepdims=True)


def gathered(block, axis, parts):
    copies = jnp.broadcast_to(block[None], (parts,) + block.shape)
    received = lax.all_to_all(copies, axis, 0, 0, tiled=True)
    return received.reshape((parts * block.shape[0],) + block.shape[1:])


def summed_over(partial, axis, parts, sent_as):
    pieces = partial.astype(sent_as).reshape((parts, partial.shape[0] // parts) + partial.shape[1:])
    received = lax.all_to_all(pieces, axis, 0, 0, tiled=True)
    return jnp.sum(received.astype(jnp.float32), 0)


def guarded(tile_work, operands):
    return tile_work(*operands)


def local(inputs, q_raw, grad_out, segments, w_key, w_value, q_gain, k_gain, row_parts, col_parts):
    tokens_here = inputs[0]
    tok_rows = tokens_here.shape[0]
    kv_width = w_key.shape[2]
    kv_heads = kv_width // HEAD
    q_heads = q_raw.shape[2] // HEAD
    group = q_heads // kv_heads
    score_scale = HEAD ** (-0.5)
    reach_blocks = WINDOW // tok_rows
    col_index = lax.axis_index("cz")
    ctx_index = lax.axis_index("cb") * col_parts + col_index
    both_rows = jnp.concatenate([w_key[0], w_value[0]], 1)
    weight_slice = lax.all_gather(both_rows, "cz", axis=0, tiled=True)
    inputs_slice = lax.all_to_all(tokens_here, "cb", 1, 0, tiled=True)
    projected = summed_over(
        jnp.dot(inputs_slice, weight_slice, preferred_element_type=jnp.float32),
        "cb",
        row_parts,
        jnp.bfloat16,
    )
    key_raw = projected[:, :kv_width].astype(jnp.bfloat16)
    value_own = projected[:, kv_width:].astype(jnp.bfloat16).reshape(tok_rows, kv_heads, HEAD)
    local_pos = jnp.arange(tok_rows, dtype=jnp.int32)
    positions = ctx_index * tok_rows + local_pos
    cosine, sine_table = rope_tables(positions)
    query_in = q_raw[0].astype(jnp.float32).reshape(tok_rows, q_heads, HEAD)
    query_norm, query_inv = normalize(query_in, q_gain[0])
    query_rot = rotate(query_norm, cosine, sine_table).astype(jnp.bfloat16)
    key_in = key_raw.astype(jnp.float32).reshape(tok_rows, kv_heads, HEAD)
    key_norm, key_inv = normalize(key_in, k_gain[0])
    key_rot = rotate(key_norm, cosine, sine_table).astype(jnp.bfloat16)
    own_pair = jnp.stack([key_rot, value_own])
    key_blocks = [own_pair]
    for distance in range(1, reach_blocks + 1):
        key_blocks.append(passed_along(own_pair, CTX, distance))
    seg_all = segments[0]
    seg_query = lax.dynamic_slice_in_dim(seg_all, ctx_index * tok_rows, tok_rows)
    allowed_list = []
    for distance in range(reach_blocks + 1):
        key_pos = (ctx_index - distance) * tok_rows + local_pos
        seg_key = lax.dynamic_slice_in_dim(
            seg_all, jnp.maximum(ctx_index - distance, 0) * tok_rows, tok_rows
        )
        offset = positions[:, None] - key_pos[None, :]
        allowed = (
            (offset >= 0)
            & (offset < WINDOW)
            & (key_pos >= 0)[None, :]
            & (seg_query[:, None] == seg_key[None, :])
        )
        allowed_list.append(allowed)
    q_group = query_rot.reshape(tok_rows, kv_heads, group, HEAD)
    out_grad = grad_out[0].reshape(tok_rows, kv_heads, group, HEAD)

    def exp_block(key_pair, allowed):
        scores = (
            jnp.einsum("qgrd,kgd->grqk", q_group, key_pair[0], preferred_element_type=jnp.float32)
            * score_scale
        )
        return jnp.where(allowed, jnp.exp(scores), 0.0)

    def total_block(key_pair, allowed):
        return jnp.sum(exp_block(key_pair, allowed), -1)

    zero_total = jnp.zeros((kv_heads, group, tok_rows), jnp.float32)
    row_total = zero_total
    for distance in range(reach_blocks + 1):
        row_total = row_total + guarded(total_block, (key_blocks[distance], allowed_list[distance]))

    def prob_block(key_pair, allowed):
        prob_tile = (exp_block(key_pair, allowed) / row_total[..., None]).astype(jnp.bfloat16)
        out_tile = jnp.einsum(
            "grqk,kgd->qgrd", prob_tile, key_pair[1], preferred_element_type=jnp.float32
        )
        return (prob_tile, out_tile)

    zero_query = jnp.zeros((tok_rows, kv_heads, group, HEAD), jnp.float32)
    prob_list = []
    attn_out = zero_query
    for distance in range(reach_blocks + 1):
        prob_tile, out_tile = guarded(prob_block, (key_blocks[distance], allowed_list[distance]))
        prob_list.append(prob_tile)
        attn_out = attn_out + out_tile
    row_delta = jnp.sum(out_grad.astype(jnp.float32) * attn_out, -1).transpose(1, 2, 0)[..., None]

    def grad_block(key_pair, prob_tile):
        prob_grad = jnp.einsum(
            "qgrd,kgd->grqk", out_grad, key_pair[1], preferred_element_type=jnp.float32
        )
        score_grad = (prob_tile.astype(jnp.float32) * (prob_grad - row_delta)).astype(jnp.bfloat16)
        value_grad = jnp.einsum(
            "grqk,qgrd->kgd", prob_tile, out_grad, preferred_element_type=jnp.float32
        )
        key_grad = (
            jnp.einsum("grqk,qgrd->kgd", score_grad, q_group, preferred_element_type=jnp.float32)
            * score_scale
        )
        return (score_grad, jnp.stack([key_grad, value_grad]))

    zero_pair = jnp.zeros((2, tok_rows, kv_heads, HEAD), jnp.float32)
    kv_total = zero_pair
    score_list = []
    for distance in range(reach_blocks + 1):
        score_grad, kv_part = guarded(grad_block, (key_blocks[distance], prob_list[distance]))
        score_list.append(score_grad)
        if distance == 0:
            kv_total = kv_part
        else:
            returned = passed_along(kv_part.astype(jnp.bfloat16), CTX, -distance)
            kv_total = kv_total + returned.astype(jnp.float32)
    key_back = normalize_back(key_in, key_inv, k_gain[0], unrotate(kv_total[0], cosine, sine_table))
    key_back = key_back.reshape(tok_rows, kv_width).astype(jnp.bfloat16)
    value_back = kv_total[1].reshape(tok_rows, kv_width).astype(jnp.bfloat16)
    both_back = jnp.concatenate([key_back, value_back], 1)
    group_back = gathered(both_back, "cb", row_parts)
    group_back = with_layout_constraint(group_back, Layout(major_to_minor=(0, 1)))
    weight_part = lax.dot_general(
        inputs_slice, group_back, (((0,), (0,)), ((), ())), preferred_element_type=jnp.float32
    )
    weight_part = with_layout_constraint(weight_part, Layout(major_to_minor=(0, 1)))
    weight_part, group_back = lax.optimization_barrier((weight_part, group_back))
    grad_rows = lax.psum_scatter(weight_part, "cz", scatter_dimension=0, tiled=True)
    slice_grad = lax.dot_general(
        group_back, weight_slice, (((1,), (1,)), ((), ())), preferred_element_type=jnp.float32
    ).astype(jnp.bfloat16)
    score_list, slice_grad = lax.optimization_barrier((score_list, slice_grad))
    input_grad = lax.all_to_all(
        slice_grad.reshape(row_parts, tok_rows, slice_grad.shape[1]), "cb", 0, 0, tiled=True
    )
    query_rot_grad = zero_query
    for distance in range(reach_blocks + 1):
        query_part = (
            jnp.einsum(
                "grqk,kgd->qgrd",
                score_list[distance],
                key_blocks[distance][0],
                preferred_element_type=jnp.float32,
            )
            * score_scale
        )
        query_rot_grad = query_rot_grad + query_part
    query_grad = normalize_back(
        query_in,
        query_inv,
        q_gain[0],
        unrotate(query_rot_grad.reshape(tok_rows, q_heads, HEAD), cosine, sine_table),
    )
    query_grad = query_grad.reshape(tok_rows, q_heads * HEAD).astype(jnp.bfloat16)
    passed = shifted(input_grad, "pipe", -1).transpose(1, 0, 2).reshape(tok_rows, -1)
    return (
        query_grad[None],
        grad_rows[:, :kv_width][None],
        grad_rows[:, kv_width:][None],
        passed[None],
    )


CTX = ("cb", "cz")


def solution(mesh):
    col_parts = 8
    row_parts = mesh.shape["ctx"] // col_parts
    grid = mesh.devices.reshape(row_parts, col_parts, mesh.shape["pipe"])
    split_mesh = Mesh(grid, ("cb", "cz", "pipe"))
    rows = P("pipe", CTX, None)
    inner = jax.shard_map(
        functools.partial(local, row_parts=row_parts, col_parts=col_parts),
        mesh=split_mesh,
        in_specs=(rows, rows, rows, P("pipe", None), rows, rows, P("pipe", None), P("pipe", None)),
        out_specs=(rows, rows, rows, rows),
        check_vma=False,
    )
    placed = NamedSharding(mesh, P("pipe", "ctx", None))

    def run(*args):
        return tuple(lax.with_sharding_constraint(out, placed) for out in inner(*args))

    return run
```
